32 devices in a mesh: region: 2 (over x), east: 8 (over z, y), north: 2 (over core).
Axes of the slice: x: 2, y: 2, z: 4, core: 2. Of those that a mesh axis runs over, the one named last changes fastest.
Arguments:
- photos: bfloat16 [1024, 4, 16384], P(('region', 'east', 'north')), parts along dimension 0, may hold values from -6 to 6
- footprint: int32 [1024, 1], P(('region', 'east', 'north')), parts along dimension 0, may hold values from 0 to 15; in each aligned block of 32 rows (0 to 31, 32 to 63, ...) at most 2 rows name the same one
- placement: int32 [1024], P(('region', 'east', 'north')), parts along dimension 0, may hold values from 0 to 15
- mask_rows: int32 [1024, 2], P(('region', 'east', 'north')), parts along dimension 0, may hold values from 0 to 128, as said below
- tile_scale: bfloat16 [1024], P(('region', 'east', 'north')), parts along dimension 0, may hold values from 0.5 to 2
Outputs:
- band_zero: bfloat16 [4, 2048, 4096], P(None, ('region', 'north'), 'east'), parts along dimension 1
- band_one: bfloat16 [4, 1024, 2048], P(None, ('region', 'north'), 'east'), parts along dimension 1
- band_two: bfloat16 [4, 512, 1024], P(None, ('region', 'north'), 'east'), parts along dimension 1
- band_three: bfloat16 [4, 256, 512], P(None, 'region'), parts along dimension 1
- apex: bfloat16 [4, 128, 256], P(None, 'region'), parts along dimension 1
The draws below stay inside these ranges and needn't reach their ends.
There are 2 independent parts, one for each index of `region`. The reference program is written for one: setup_inputs(seed, part) draws one part's arguments, and reference() takes and returns one part's arrays. A program takes and returns all parts, laid end to end along the dimension named above; each array names one. Nothing has to cross between parts.
Inputs may be any that keep to these rules, and one draw needn't show every extreme that they name: `footprint`: among the 32 rows of one device no tile is named more than 2 times. `mask_rows`: each row holds a first row below one past the last row.
All inputs are finite; a program needn't handle non-finite values.
Results may differ from the reference program's by a relative error of at most 0.001.
Values may be sent and summed in bfloat16 or wider, within the bound.
No kernel may reach another device: no remote copies, remote signals or barrier semaphores. Data moves between devices by JAX's collectives and lax.ppermute only.
A program may use at most 128 MiB of HBM per device.

```python
import math
import jax
import jax.numpy as jnp
import numpy as np

BANDS = 4
PATCH = 128
TILE = 512
P_DEV = 32
CAP = 2
BLOCKS = 16
OWNERS = 16
PHOTOS = 512
ROWS = 1024
COLS = 4096
N_EAST = 8
N_NORTH = 2


def draw_mask_rows(key, part):
    first_key = jax.random.fold_in(key, 11)
    second_key = jax.random.fold_in(key, 23)
    lower_row = jax.random.randint(first_key, (PHOTOS,), 0, PATCH // 4)
    upper_row = PATCH - jax.random.randint(second_key, (PHOTOS,), 0, PATCH // 4)
    leading = jnp.arange(PHOTOS) == 0
    lower_row = jnp.where(leading, 0, lower_row)
    upper_row = jnp.where(leading, PATCH, upper_row)
    return jnp.stack([lower_row, upper_row], axis=1).astype(jnp.int32)


def with_ends(values, key, smallest, top_value):
    longest = values.shape.index(max(values.shape))
    spots = []
    for shift in (0, 1):
        where = [jax.random.randint(jax.random.fold_in(key, axis), (), 0, length) for axis, length in enumerate(values.shape)]
        where[longest] = (where[longest] + shift) % values.shape[longest]
        spots.append(tuple(where))
    return values.at[spots[0]].set(smallest).at[spots[1]].set(top_value)


def block_levels(stream_key, shape, pieces, low, high):
    def one(dim, blocks):
        heights = jax.random.uniform(jax.random.fold_in(jax.random.fold_in(stream_key, 6), dim), (blocks,), jnp.float32, low / len(pieces), high / len(pieces))
        return jnp.repeat(jnp.exp(heights), shape[dim] // blocks).reshape((-1,) + (1,) * (len(shape) - dim - 1))

    factor_of = one(*pieces[0])
    for cut in pieces[1:]:
        factor_of = factor_of * one(*cut)
    return factor_of


def routed_block(own_key, own, number, rows, amount, top, bound, lean):
    order = jax.random.permutation(own_key, amount)
    packed, common = shares(amount, rows * top, bound, lean, True), shares(amount, rows * top, bound, lean, False)
    places = jnp.arange(amount)

    def named(sizes, turn):
        used = int((sizes > 0).sum())
        fixed = max(1, used // 4)
        passed = fixed + (places - fixed + turn * (used - fixed)) % max(1, amount - fixed)
        return jnp.zeros((amount,), jnp.int32).at[order[jnp.where(places < fixed, places, passed)]].set(jnp.asarray(sizes, jnp.int32))

    sizes = jnp.where(number % 4 == 0, named(packed, number // 4), named(common, number - number // 4 - 1))
    mixed = jax.random.permutation(jax.random.fold_in(own, 3), amount)
    donor, sink = mixed[0:amount // 2 * 2:2], mixed[1:amount // 2 * 2:2]
    slack = jnp.minimum(sizes[donor] - 1, bound - sizes[sink]) // 2
    slack = jnp.where((donor == order[0]) | (sink == order[0]) | (sizes[sink] == 0), 0, jnp.maximum(slack, 0))
    passed = jax.random.randint(jax.random.fold_in(own, 4), (amount // 2,), 0, 1 << 20) % (slack + 1)
    sizes = sizes.at[donor].add(-passed).at[sink].add(passed)
    labels = jnp.searchsorted(jnp.cumsum(sizes), jnp.arange(rows * top), side="right").astype(jnp.int32)
    table = labels.reshape(top, rows).T
    table = table[jax.random.permutation(jax.random.fold_in(own, 1), rows)]
    turn = jax.random.randint(jax.random.fold_in(own, 2), (rows, 1), 0, top)
    return jnp.take_along_axis(table, (jnp.arange(top)[None, :] + turn) % top, axis=1)


def shares(count, total, most, slope, full):
    weights = [(1 << 20) // math.isqrt(rank ** slope) + 1 for rank in range(1, count + 1)]
    largest = most if full else min(most, max(-(-total // count), total * weights[0] // sum(weights)))
    least = 1 if total - largest >= count - 1 else 0
    holding, spare = [largest] + [least] * (count - 1), total - largest - least * (count - 1)
    while spare > 0:
        candidates = [i for i in range(1, count) if holding[i] < largest] or [i for i in range(1, count) if holding[i] < most]
        mass, left = sum([weights[i] for i in candidates]), spare
        for i in candidates:
            addition = min(most - holding[i], max(1, left * weights[i] // mass), spare)
            holding[i] = holding[i] + addition
            spare = spare - addition
    return np.array(holding)


def gaussian(rng, dims, width, limit, shards=(), held_as=jnp.bfloat16):
    gain = block_levels(rng, dims, shards, -0.22, 0.18) if shards else 1.0
    drawn = jax.random.normal(rng, dims, jnp.float32) * width * gain
    return jnp.minimum(jnp.maximum(drawn, -limit), limit).astype(held_as)


def setup_inputs(seed: int = 0, part: int = 0) -> dict:
    seeds = jax.random.split(jax.random.key(seed), 6)
    own_keys = jax.random.split(jax.random.fold_in(seeds[5], part), 6)
    photos = gaussian(own_keys[0], (PHOTOS, BANDS, PATCH * PATCH), 1.0, 6.0, ((0, 16),))
    footprint_keys = jax.random.split(jax.random.fold_in(own_keys[1], 1), PHOTOS // P_DEV)
    footprint_turns = jax.random.permutation(jax.random.fold_in(own_keys[1], 3), PHOTOS // P_DEV)
    footprint = jax.vmap(lambda own, number: routed_block(jax.random.fold_in(own_keys[1], 2), own, number, P_DEV, OWNERS, 1, CAP, 2))(footprint_keys, footprint_turns).reshape((PHOTOS, 1))
    placement = with_ends(jax.random.randint(own_keys[2], (PHOTOS,), 0, BLOCKS), jax.random.fold_in(own_keys[2], 1), 0, BLOCKS - 1).astype(jnp.int32)
    mask_rows = draw_mask_rows(jax.random.fold_in(jax.random.fold_in(seeds[5], part), 71), part)
    tile_scale = jnp.clip(jnp.exp(math.log(2.0) - 1.3862944 * jax.random.uniform(own_keys[4], (PHOTOS,), jnp.float32) ** block_levels(own_keys[4], (PHOTOS,), ((0, 16),), -0.2, 0.2)), 0.5, 2.0).astype(jnp.bfloat16)
    return dict(photos=photos, footprint=footprint, placement=placement, mask_rows=mask_rows, tile_scale=tile_scale)


KERNEL = (0.0625, 0.25, 0.375, 0.25, 0.0625)
FLOOR = 0.1


def blur_rows(padded, extent):
    running = KERNEL[0] * padded[:, 0:extent, :]
    for tap_index in range(1, 5):
        running = running + KERNEL[tap_index] * padded[:, tap_index:tap_index + extent, :]
    return running


def blur_cols(padded, extent):
    running = KERNEL[0] * padded[:, :, 0:extent]
    for tap_index in range(1, 5):
        running = running + KERNEL[tap_index] * padded[:, :, tap_index:tap_index + extent]
    return running


def smooth(grid_field):
    tall_size = grid_field.shape[1]
    wide_size = grid_field.shape[2]
    padded = jnp.pad(grid_field, ((0, 0), (2, 2), (2, 2)))
    return blur_cols(blur_rows(padded, tall_size), wide_size)


def spread(coarse):
    chan_count, tall_size, wide_size = coarse.shape
    rows_done = jnp.stack([coarse, jnp.zeros_like(coarse)], axis=2).reshape(chan_count, 2 * tall_size, wide_size)
    return jnp.stack([rows_done, jnp.zeros_like(rows_done)], axis=3).reshape(chan_count, 2 * tall_size, 2 * wide_size)


def normalize(grid_field):
    return grid_field[:-1] / jnp.maximum(grid_field[-1:], FLOOR)


def expand(coarse):
    return 4.0 * smooth(spread(coarse))


def reference(photos, footprint, placement, mask_rows, tile_scale):
    photo_count = photos.shape[0]
    side_index = jnp.arange(PATCH, dtype=jnp.int32)
    edge_weight = (1 + jnp.minimum(side_index, PATCH - 1 - side_index)).astype(jnp.float32)
    feather = edge_weight[:, None] * edge_weight[None, :] / float((PATCH // 2) ** 2)
    lower_row = mask_rows[:, 0:1]
    upper_row = mask_rows[:, 1:2]
    inside = ((side_index[None, :] >= lower_row) & (side_index[None, :] < upper_row)).astype(jnp.float32)
    weight = (inside[:, :, None] * feather[None, :, :]).reshape(photo_count, PATCH * PATCH)
    gain_value = tile_scale.astype(jnp.float32)[:, None] * weight
    weighted = photos.astype(jnp.float32) * gain_value[:, None, :]
    contribution = jnp.concatenate([weighted, weight[:, None, :]], axis=1)
    segment = (footprint[:, 0] * BLOCKS + placement).astype(jnp.int32)
    summed = jax.ops.segment_sum(contribution, segment, num_segments=OWNERS * BLOCKS)
    side_blocks = TILE // PATCH
    canvas = summed.reshape(N_EAST, N_NORTH, side_blocks, side_blocks, BANDS + 1, PATCH, PATCH)
    canvas = canvas.transpose(4, 1, 2, 5, 0, 3, 6).reshape(BANDS + 1, ROWS, COLS)
    level_field = canvas
    results = []
    for depth_step in range(4):
        coarse = smooth(level_field)[:, ::2, ::2]
        laplace_band = normalize(level_field) - expand(normalize(coarse))
        results.append(laplace_band.astype(jnp.bfloat16))
        level_field = coarse
    apex = normalize(level_field).astype(jnp.bfloat16)
    return (results[0], results[1], results[2], results[3], apex)
```

```python
import jax
import jax.numpy as jnp
from jax import lax
from jax.sharding import PartitionSpec as P

BANDS = 4
PATCH = 128
TILE = 512
CAP = 2
BLOCKS = 16


KERNEL = (0.0625, 0.25, 0.375, 0.25, 0.0625)
FLOOR = 0.1
MARGINS = (22, 10, 4, 1)


def padded_2(block, sides, width):
    for axis, dim in sides:
        count = lax.axis_size(axis)
        forward = [(i, i + 1) for i in range(count - 1)]
        backward = [(target, source) for source, target in forward]
        low = lax.ppermute(
            lax.slice_in_dim(block, block.shape[dim] - width, None, axis=dim), axis, forward
        )
        high = lax.ppermute(lax.slice_in_dim(block, 0, width, axis=dim), axis, backward)
        block = jnp.concatenate([low, block, high], axis=dim)
    return block


def tap_table(offset, scale):
    table = jnp.zeros(offset.shape, jnp.float32)
    for tap_index in range(5):
        table = table + jnp.where(offset == tap_index, scale * KERNEL[tap_index], 0.0)
    return table.astype(jnp.bfloat16)


def split_einsum(spec, first, second, table_first):
    field = second if table_first else first
    spread_field = field * 65537.0
    high = spread_field - (spread_field - field)
    low = field - high
    both = jnp.concatenate([high, low], axis=0).astype(jnp.bfloat16)
    pair = (first, both) if table_first else (both, second)
    term = jnp.einsum(spec, *pair, preferred_element_type=jnp.float32)
    chan_count = field.shape[0]
    return term[:chan_count] + term[chan_count:]


def reduce_table(size_in):
    size_out = (size_in - 3) // 2
    out_index = jnp.arange(size_out, dtype=jnp.int32)
    in_index = jnp.arange(size_in, dtype=jnp.int32)
    return tap_table(in_index[None, :] - 2 * out_index[:, None], 1.0)


def expand_table(size_in):
    size_out = 2 * (size_in - 2)
    out_index = jnp.arange(size_out, dtype=jnp.int32)
    in_index = jnp.arange(size_in, dtype=jnp.int32)
    return tap_table(2 * in_index[None, :] - out_index[:, None], 2.0)


def apply_tables(padded, row_table, col_table):
    rows_done = split_einsum("ih,chw->ciw", row_table, padded, True)
    return split_einsum("ciw,jw->cij", rows_done, col_table, False)


def reduce_padded(padded):
    return apply_tables(padded, reduce_table(padded.shape[1]), reduce_table(padded.shape[2]))


def expand_padded(padded):
    return apply_tables(padded, expand_table(padded.shape[1]), expand_table(padded.shape[2]))


def normalize(grid_field):
    return grid_field[:-1] / jnp.maximum(grid_field[-1:], FLOOR)


def crop_margin(grid_field, margin, keep):
    cut = margin - keep
    return grid_field[:, cut : grid_field.shape[1] - cut, cut : grid_field.shape[2] - cut]


def mask_region(grid_field, margin, tile_side, north_pos, east_pos, north_count, east_count):
    row_global = north_pos * tile_side + jnp.arange(grid_field.shape[1], dtype=jnp.int32) - margin
    col_global = east_pos * tile_side + jnp.arange(grid_field.shape[2], dtype=jnp.int32) - margin
    row_keep = (row_global >= 0) & (row_global < north_count * tile_side)
    col_keep = (col_global >= 0) & (col_global < east_count * tile_side)
    keep_table = (row_keep[:, None] & col_keep[None, :]).astype(jnp.float32)
    return grid_field * keep_table[None, :, :]


def body(photos, footprint, placement, mask_rows, tile_scale):
    east_count = lax.axis_size("east")
    north_count = lax.axis_size("north")
    owners = east_count * north_count
    photo_count = photos.shape[0]
    slot_total = owners * CAP
    target = footprint[:, 0]
    member_table = (target[:, None] == jnp.arange(owners, dtype=jnp.int32)[None, :]).astype(
        jnp.int32
    )
    earlier_count = jnp.cumsum(member_table, axis=0) - member_table
    place_rank = jnp.sum(earlier_count * member_table, axis=1)
    slot_index = target * CAP + place_rank
    slot_match = slot_index[None, :] == jnp.arange(slot_total, dtype=jnp.int32)[:, None]
    filled = jnp.any(slot_match, axis=1)
    source = jnp.sum(
        jnp.where(slot_match, jnp.arange(photo_count, dtype=jnp.int32)[None, :], 0), axis=1
    )
    record = jnp.stack(
        [
            tile_scale.astype(jnp.float32),
            placement.astype(jnp.float32),
            mask_rows[:, 0].astype(jnp.float32),
            mask_rows[:, 1].astype(jnp.float32),
            jnp.ones((photo_count,), jnp.float32),
        ],
        axis=1,
    ).astype(jnp.bfloat16)
    pixel_total = BANDS * PATCH * PATCH
    payload = jnp.concatenate(
        [
            photos.reshape(photo_count, pixel_total),
            jnp.pad(record, ((0, 0), (0, PATCH - record.shape[1]))),
        ],
        axis=1,
    )
    pick = slot_match.astype(jnp.bfloat16)
    send = jnp.einsum("sp,pj->sj", pick, payload, preferred_element_type=jnp.float32).astype(
        jnp.bfloat16
    )
    got = lax.all_to_all(send, ("east", "north"), split_axis=0, concat_axis=0, tiled=True)
    got_photos = got[:, :pixel_total]
    record_value = got[:, pixel_total : pixel_total + 5].astype(jnp.float32)
    gain_scale = record_value[:, 0]
    block_index = record_value[:, 1].astype(jnp.int32)
    lower_row = record_value[:, 2:3]
    upper_row = record_value[:, 3:4]
    live_flag = record_value[:, 4]
    side_index = jnp.arange(PATCH, dtype=jnp.int32)
    edge_weight = (1 + jnp.minimum(side_index, PATCH - 1 - side_index)).astype(jnp.float32)
    feather = edge_weight[:, None] * edge_weight[None, :] / float((PATCH // 2) ** 2)
    side_float = side_index.astype(jnp.float32)
    inside = ((side_float[None, :] >= lower_row) & (side_float[None, :] < upper_row)).astype(
        jnp.float32
    ) * live_flag[:, None]
    weight = inside[:, :, None] * feather[None, :, :]
    gain_value = gain_scale[:, None, None] * weight
    window_photos = got_photos.reshape(slot_total, BANDS, PATCH, PATCH)
    weighted = window_photos.astype(jnp.float32) * gain_value[:, None, :, :]
    block_match = (block_index[None, :] == jnp.arange(BLOCKS, dtype=jnp.int32)[:, None]).astype(
        jnp.float32
    )
    band_sums = jnp.einsum(
        "bk,kcrs->bcrs",
        block_match,
        weighted,
        precision=lax.Precision.HIGHEST,
        preferred_element_type=jnp.float32,
    )
    weight_sums = jnp.einsum(
        "bk,krs->brs",
        block_match,
        weight,
        precision=lax.Precision.HIGHEST,
        preferred_element_type=jnp.float32,
    )
    summed = jnp.concatenate([band_sums, weight_sums[:, None]], axis=1)
    side_blocks = TILE // PATCH
    strips = []
    for block_row in range(side_blocks):
        strips.append(
            jnp.concatenate(
                [summed[block_row * side_blocks + block_col] for block_col in range(side_blocks)],
                axis=2,
            )
        )
    canvas = jnp.concatenate(strips, axis=1)
    results = []
    east_pos = lax.axis_index("east")
    north_pos = lax.axis_index("north")
    levels = [padded_2(canvas, (("east", 2), ("north", 1)), MARGINS[0])]
    for depth_step in range(3):
        coarse = reduce_padded(levels[-1])
        levels.append(
            mask_region(
                coarse,
                MARGINS[depth_step + 1],
                TILE >> depth_step + 1,
                north_pos,
                east_pos,
                north_count,
                east_count,
            )
        )
    level_field = crop_margin(levels[3], MARGINS[3], 0)
    stacked = lax.all_gather(level_field[None], ("east", "north"), axis=0, tiled=True)
    for depth_step in range(3):
        own_field = crop_margin(levels[depth_step], MARGINS[depth_step], 0)
        coarse_normal = normalize(crop_margin(levels[depth_step + 1], MARGINS[depth_step + 1], 1))
        laplace_band = normalize(own_field) - expand_padded(coarse_normal)
        results.append(laplace_band.astype(jnp.bfloat16))
    chan_count, tall_size, wide_size = level_field.shape
    whole_field = stacked.reshape(east_count, north_count, chan_count, tall_size, wide_size)
    whole_field = whole_field.transpose(2, 1, 3, 0, 4).reshape(
        chan_count, north_count * tall_size, east_count * wide_size
    )
    top_field = reduce_padded(jnp.pad(whole_field, ((0, 0), (2, 2), (2, 2))))
    top_normal = normalize(top_field)
    band_three = (
        normalize(whole_field) - expand_padded(jnp.pad(top_normal, ((0, 0), (1, 1), (1, 1))))
    ).astype(jnp.bfloat16)
    apex = top_normal.astype(jnp.bfloat16)
    return (results[0], results[1], results[2], band_three, apex)


def solution(mesh):
    return jax.shard_map(
        body,
        mesh=mesh,
        in_specs=(
            P(("region", "east", "north"), None, None),
            P(("region", "east", "north"), None),
            P(("region", "east", "north")),
            P(("region", "east", "north"), None),
            P(("region", "east", "north")),
        ),
        out_specs=(
            P(None, ("region", "north"), "east"),
            P(None, ("region", "north"), "east"),
            P(None, ("region", "north"), "east"),
            P(None, "region", None),
            P(None, "region", None),
        ),
        check_vma=False,
    )
```

```python
import jax
import jax.numpy as jnp
from jax import lax
from jax.sharding import PartitionSpec as P

BANDS = 4
PATCH = 128
TILE = 512
CAP = 2
BLOCKS = 16


KERNEL = (0.0625, 0.25, 0.375, 0.25, 0.0625)
FLOOR = 0.1
MARGINS = (22, 10, 4, 1)


def padded_2(block, sides, width):
    for axis, dim in sides:
        count = lax.axis_size(axis)
        forward = [(i, i + 1) for i in range(count - 1)]
        backward = [(target, source) for source, target in forward]
        low = lax.ppermute(
            lax.slice_in_dim(block, block.shape[dim] - width, None, axis=dim), axis, forward
        )
        high = lax.ppermute(lax.slice_in_dim(block, 0, width, axis=dim), axis, backward)
        block = jnp.concatenate([low, block, high], axis=dim)
    return block


def tap_table(offset, scale):
    table = jnp.zeros(offset.shape, jnp.float32)
    for tap_index in range(5):
        table = table + jnp.where(offset == tap_index, scale * KERNEL[tap_index], 0.0)
    return table.astype(jnp.bfloat16)


def split_einsum(spec, first, second, table_first):
    field = second if table_first else first
    spread_field = field * 65537.0
    high = spread_field - (spread_field - field)
    low = field - high
    both = jnp.concatenate([high, low], axis=0).astype(jnp.bfloat16)
    pair = (first, both) if table_first else (both, second)
    term = jnp.einsum(spec, *pair, preferred_element_type=jnp.float32)
    chan_count = field.shape[0]
    return term[:chan_count] + term[chan_count:]


def reduce_table(size_in):
    size_out = (size_in - 3) // 2
    out_index = jnp.arange(size_out, dtype=jnp.int32)
    in_index = jnp.arange(size_in, dtype=jnp.int32)
    return tap_table(in_index[None, :] - 2 * out_index[:, None], 1.0)


def expand_table(size_in):
    size_out = 2 * (size_in - 2)
    out_index = jnp.arange(size_out, dtype=jnp.int32)
    in_index = jnp.arange(size_in, dtype=jnp.int32)
    return tap_table(2 * in_index[None, :] - out_index[:, None], 2.0)


def apply_tables(padded, row_table, col_table):
    rows_done = split_einsum("ih,chw->ciw", row_table, padded, True)
    return split_einsum("ciw,jw->cij", rows_done, col_table, False)


def reduce_padded(padded):
    return apply_tables(padded, reduce_table(padded.shape[1]), reduce_table(padded.shape[2]))


def expand_padded(padded):
    return apply_tables(padded, expand_table(padded.shape[1]), expand_table(padded.shape[2]))


def normalize(grid_field):
    return grid_field[:-1] / jnp.maximum(grid_field[-1:], FLOOR)


def crop_margin(grid_field, margin, keep):
    cut = margin - keep
    return grid_field[:, cut : grid_field.shape[1] - cut, cut : grid_field.shape[2] - cut]


def mask_region(grid_field, margin, tile_side, north_pos, east_pos, north_count, east_count):
    row_global = north_pos * tile_side + jnp.arange(grid_field.shape[1], dtype=jnp.int32) - margin
    col_global = east_pos * tile_side + jnp.arange(grid_field.shape[2], dtype=jnp.int32) - margin
    row_keep = (row_global >= 0) & (row_global < north_count * tile_side)
    col_keep = (col_global >= 0) & (col_global < east_count * tile_side)
    keep_table = (row_keep[:, None] & col_keep[None, :]).astype(jnp.float32)
    return grid_field * keep_table[None, :, :]


def add_borders(field):
    for axis, dim in (("east", 2), ("north", 1)):
        count = lax.axis_size(axis)
        forward = [(i, i + 1) for i in range(count - 1)]
        backward = [(target, source) for source, target in forward]
        size = field.shape[dim]
        from_low = lax.ppermute(lax.slice_in_dim(field, size - 3, size, axis=dim), axis, forward)
        from_high = lax.ppermute(lax.slice_in_dim(field, 0, 3, axis=dim), axis, backward)
        pad_low = [(0, 0)] * 3
        pad_high = [(0, 0)] * 3
        pad_low[dim] = (1, size - 4)
        pad_high[dim] = (size - 4, 1)
        field = field + jnp.pad(from_low, pad_low) + jnp.pad(from_high, pad_high)
    return crop_margin(field, 2, 1)


def overlap_add(stacked, east_count, north_count):
    chan_count, tall_span, wide_span = stacked.shape[1:]
    tiles = stacked.reshape(east_count, north_count, chan_count, tall_span, wide_span)
    for tile_axis, dim in ((0, 4), (1, 3)):
        span = tiles.shape[dim]
        core = lax.slice_in_dim(tiles, 2, span - 2, axis=dim)
        low_spill = lax.slice_in_dim(tiles, 0, 2, axis=dim)
        high_spill = lax.slice_in_dim(tiles, span - 2, span, axis=dim)
        count = tiles.shape[tile_axis]
        zero = jnp.zeros_like(lax.slice_in_dim(low_spill, 0, 1, axis=tile_axis))
        into_last = jnp.concatenate(
            [lax.slice_in_dim(low_spill, 1, count, axis=tile_axis), zero], axis=tile_axis
        )
        into_first = jnp.concatenate(
            [zero, lax.slice_in_dim(high_spill, 0, count - 1, axis=tile_axis)], axis=tile_axis
        )
        inner = span - 4
        pad_first = [(0, 0)] * 5
        pad_last = [(0, 0)] * 5
        pad_first[dim] = (0, inner - 2)
        pad_last[dim] = (inner - 2, 0)
        tiles = core + jnp.pad(into_first, pad_first) + jnp.pad(into_last, pad_last)
    tall_size, wide_size = tiles.shape[3], tiles.shape[4]
    return tiles.transpose(2, 1, 3, 0, 4).reshape(
        chan_count, north_count * tall_size, east_count * wide_size
    )


def body(photos, footprint, placement, mask_rows, tile_scale):
    east_count = lax.axis_size("east")
    north_count = lax.axis_size("north")
    owners = east_count * north_count
    photo_count = photos.shape[0]
    slot_total = owners * CAP
    target = footprint[:, 0]
    member_table = (target[:, None] == jnp.arange(owners, dtype=jnp.int32)[None, :]).astype(
        jnp.int32
    )
    earlier_count = jnp.cumsum(member_table, axis=0) - member_table
    place_rank = jnp.sum(earlier_count * member_table, axis=1)
    slot_index = target * CAP + place_rank
    slot_match = slot_index[None, :] == jnp.arange(slot_total, dtype=jnp.int32)[:, None]
    filled = jnp.any(slot_match, axis=1)
    source = jnp.sum(
        jnp.where(slot_match, jnp.arange(photo_count, dtype=jnp.int32)[None, :], 0), axis=1
    )
    record = jnp.stack(
        [
            tile_scale.astype(jnp.float32),
            placement.astype(jnp.float32),
            mask_rows[:, 0].astype(jnp.float32),
            mask_rows[:, 1].astype(jnp.float32),
            jnp.ones((photo_count,), jnp.float32),
        ],
        axis=1,
    ).astype(jnp.bfloat16)
    pixel_total = BANDS * PATCH * PATCH
    payload = jnp.concatenate(
        [
            photos.reshape(photo_count, pixel_total),
            jnp.pad(record, ((0, 0), (0, PATCH - record.shape[1]))),
        ],
        axis=1,
    )
    pick = slot_match.astype(jnp.bfloat16)
    send = jnp.einsum("sp,pj->sj", pick, payload, preferred_element_type=jnp.float32).astype(
        jnp.bfloat16
    )
    got = lax.all_to_all(send, ("east", "north"), split_axis=0, concat_axis=0, tiled=True)
    got_photos = got[:, :pixel_total]
    record_value = got[:, pixel_total : pixel_total + 5].astype(jnp.float32)
    gain_scale = record_value[:, 0]
    block_index = record_value[:, 1].astype(jnp.int32)
    lower_row = record_value[:, 2:3]
    upper_row = record_value[:, 3:4]
    live_flag = record_value[:, 4]
    side_index = jnp.arange(PATCH, dtype=jnp.int32)
    edge_weight = (1 + jnp.minimum(side_index, PATCH - 1 - side_index)).astype(jnp.float32)
    feather = edge_weight[:, None] * edge_weight[None, :] / float((PATCH // 2) ** 2)
    side_float = side_index.astype(jnp.float32)
    inside = ((side_float[None, :] >= lower_row) & (side_float[None, :] < upper_row)).astype(
        jnp.float32
    ) * live_flag[:, None]
    weight = inside[:, :, None] * feather[None, :, :]
    gain_value = gain_scale[:, None, None] * weight
    window_photos = got_photos.reshape(slot_total, BANDS, PATCH, PATCH)
    weighted = window_photos.astype(jnp.float32) * gain_value[:, None, :, :]
    block_match = (block_index[None, :] == jnp.arange(BLOCKS, dtype=jnp.int32)[:, None]).astype(
        jnp.float32
    )
    band_sums = jnp.einsum(
        "bk,kcrs->bcrs",
        block_match,
        weighted,
        precision=lax.Precision.HIGHEST,
        preferred_element_type=jnp.float32,
    )
    weight_sums = jnp.einsum(
        "bk,krs->brs",
        block_match,
        weight,
        precision=lax.Precision.HIGHEST,
        preferred_element_type=jnp.float32,
    )
    summed = jnp.concatenate([band_sums, weight_sums[:, None]], axis=1)
    side_blocks = TILE // PATCH
    strips = []
    for block_row in range(side_blocks):
        strips.append(
            jnp.concatenate(
                [summed[block_row * side_blocks + block_col] for block_col in range(side_blocks)],
                axis=2,
            )
        )
    canvas = jnp.concatenate(strips, axis=1)
    results = []
    east_pos = lax.axis_index("east")
    north_pos = lax.axis_index("north")
    own_levels = [canvas]
    spill_pad = 6
    for depth_step in range(3):
        field = jnp.pad(
            own_levels[-1], ((0, 0), (spill_pad, spill_pad), (spill_pad, spill_pad))
        )
        own_levels.append(
            mask_region(
                reduce_padded(field),
                2,
                TILE >> depth_step + 1,
                north_pos,
                east_pos,
                north_count,
                east_count,
            )
        )
        spill_pad = 4
    stacked = lax.all_gather(own_levels[3][None], ("east", "north"), axis=0, tiled=True)
    true_levels = [canvas] + [add_borders(own_levels[depth]) for depth in (1, 2, 3)]
    for depth_step in range(3):
        own_field = true_levels[depth_step]
        if depth_step:
            own_field = crop_margin(own_field, 1, 0)
        laplace_band = normalize(own_field) - expand_padded(normalize(true_levels[depth_step + 1]))
        results.append(laplace_band.astype(jnp.bfloat16))
    whole_field = overlap_add(stacked, east_count, north_count)
    top_field = reduce_padded(jnp.pad(whole_field, ((0, 0), (2, 2), (2, 2))))
    top_normal = normalize(top_field)
    band_three = (
        normalize(whole_field) - expand_padded(jnp.pad(top_normal, ((0, 0), (1, 1), (1, 1))))
    ).astype(jnp.bfloat16)
    apex = top_normal.astype(jnp.bfloat16)
    return (results[0], results[1], results[2], band_three, apex)


def solution(mesh):
    return jax.shard_map(
        body,
        mesh=mesh,
        in_specs=(
            P(("region", "east", "north"), None, None),
            P(("region", "east", "north"), None),
            P(("region", "east", "north")),
            P(("region", "east", "north"), None),
            P(("region", "east", "north")),
        ),
        out_specs=(
            P(None, ("region", "north"), "east"),
            P(None, ("region", "north"), "east"),
            P(None, ("region", "north"), "east"),
            P(None, "region", None),
            P(None, "region", None),
        ),
        check_vma=False,
    )
```

```python
import jax
import jax.numpy as jnp
from jax import lax
from jax.sharding import PartitionSpec as P

BANDS = 4
PATCH = 128
TILE = 512
CAP = 2
BLOCKS = 16


KERNEL = (0.0625, 0.25, 0.375, 0.25, 0.0625)
FLOOR = 0.1
MARGINS = (22, 10, 4, 1)


def padded_2(block, sides, width):
    for axis, dim in sides:
        count = lax.axis_size(axis)
        forward = [(i, i + 1) for i in range(count - 1)]
        backward = [(target, source) for source, target in forward]
        low = lax.ppermute(
            lax.slice_in_dim(block, block.shape[dim] - width, None, axis=dim), axis, forward
        )
        high = lax.ppermute(lax.slice_in_dim(block, 0, width, axis=dim), axis, backward)
        block = jnp.concatenate([low, block, high], axis=dim)
    return block


def tap_table(offset, scale):
    table = jnp.zeros(offset.shape, jnp.float32)
    for tap_index in range(5):
        table = table + jnp.where(offset == tap_index, scale * KERNEL[tap_index], 0.0)
    return table.astype(jnp.bfloat16)


def split_einsum(spec, first, second, table_first):
    field = second if table_first else first
    spread_field = field * 65537.0
    high = spread_field - (spread_field - field)
    low = field - high
    both = jnp.concatenate([high, low], axis=0).astype(jnp.bfloat16)
    pair = (first, both) if table_first else (both, second)
    term = jnp.einsum(spec, *pair, preferred_element_type=jnp.float32)
    chan_count = field.shape[0]
    return term[:chan_count] + term[chan_count:]


def reduce_table(size_in):
    size_out = (size_in - 3) // 2
    out_index = jnp.arange(size_out, dtype=jnp.int32)
    in_index = jnp.arange(size_in, dtype=jnp.int32)
    return tap_table(in_index[None, :] - 2 * out_index[:, None], 1.0)


def expand_table(size_in):
    size_out = 2 * (size_in - 2)
    out_index = jnp.arange(size_out, dtype=jnp.int32)
    in_index = jnp.arange(size_in, dtype=jnp.int32)
    return tap_table(2 * in_index[None, :] - out_index[:, None], 2.0)


def apply_tables(padded, row_table, col_table):
    rows_done = split_einsum("ih,chw->ciw", row_table, padded, True)
    return split_einsum("ciw,jw->cij", rows_done, col_table, False)


def reduce_padded(padded):
    return apply_tables(padded, reduce_table(padded.shape[1]), reduce_table(padded.shape[2]))


def expand_padded(padded):
    return apply_tables(padded, expand_table(padded.shape[1]), expand_table(padded.shape[2]))


def normalize(grid_field):
    return grid_field[:-1] / jnp.maximum(grid_field[-1:], FLOOR)


def crop_margin(grid_field, margin, keep):
    cut = margin - keep
    return grid_field[:, cut : grid_field.shape[1] - cut, cut : grid_field.shape[2] - cut]


def mask_region(grid_field, margin, tile_side, north_pos, east_pos, north_count, east_count):
    row_global = north_pos * tile_side + jnp.arange(grid_field.shape[1], dtype=jnp.int32) - margin
    col_global = east_pos * tile_side + jnp.arange(grid_field.shape[2], dtype=jnp.int32) - margin
    row_keep = (row_global >= 0) & (row_global < north_count * tile_side)
    col_keep = (col_global >= 0) & (col_global < east_count * tile_side)
    keep_table = (row_keep[:, None] & col_keep[None, :]).astype(jnp.float32)
    return grid_field * keep_table[None, :, :]


def add_borders(fields):
    for axis, dim in (("east", 2), ("north", 1)):
        count = lax.axis_size(axis)
        forward = [(i, i + 1) for i in range(count - 1)]
        backward = [(target, source) for source, target in forward]
        other = 3 - dim
        lows = [lax.slice_in_dim(f, f.shape[dim] - 3, f.shape[dim], axis=dim) for f in fields]
        highs = [lax.slice_in_dim(f, 0, 3, axis=dim) for f in fields]
        from_low = lax.ppermute(jnp.concatenate(lows, axis=other), axis, forward)
        from_high = lax.ppermute(jnp.concatenate(highs, axis=other), axis, backward)
        updated = []
        offset = 0
        for f in fields:
            size = f.shape[dim]
            extent = f.shape[other]
            low_part = lax.slice_in_dim(from_low, offset, offset + extent, axis=other)
            high_part = lax.slice_in_dim(from_high, offset, offset + extent, axis=other)
            offset += extent
            pad_low = [(0, 0)] * 3
            pad_high = [(0, 0)] * 3
            pad_low[dim] = (1, size - 4)
            pad_high[dim] = (size - 4, 1)
            updated.append(f + jnp.pad(low_part, pad_low) + jnp.pad(high_part, pad_high))
        fields = updated
    return [crop_margin(f, 2, 1) for f in fields]


def overlap_add(stacked, east_count, north_count):
    chan_count, tall_span, wide_span = stacked.shape[1:]
    tiles = stacked.reshape(east_count, north_count, chan_count, tall_span, wide_span)
    for tile_axis, dim in ((0, 4), (1, 3)):
        span = tiles.shape[dim]
        core = lax.slice_in_dim(tiles, 2, span - 2, axis=dim)
        low_spill = lax.slice_in_dim(tiles, 0, 2, axis=dim)
        high_spill = lax.slice_in_dim(tiles, span - 2, span, axis=dim)
        count = tiles.shape[tile_axis]
        zero = jnp.zeros_like(lax.slice_in_dim(low_spill, 0, 1, axis=tile_axis))
        into_last = jnp.concatenate(
            [lax.slice_in_dim(low_spill, 1, count, axis=tile_axis), zero], axis=tile_axis
        )
        into_first = jnp.concatenate(
            [zero, lax.slice_in_dim(high_spill, 0, count - 1, axis=tile_axis)], axis=tile_axis
        )
        inner = span - 4
        pad_first = [(0, 0)] * 5
        pad_last = [(0, 0)] * 5
        pad_first[dim] = (0, inner - 2)
        pad_last[dim] = (inner - 2, 0)
        tiles = core + jnp.pad(into_first, pad_first) + jnp.pad(into_last, pad_last)
    tall_size, wide_size = tiles.shape[3], tiles.shape[4]
    return tiles.transpose(2, 1, 3, 0, 4).reshape(
        chan_count, north_count * tall_size, east_count * wide_size
    )


def body(photos, footprint, placement, mask_rows, tile_scale):
    east_count = lax.axis_size("east")
    north_count = lax.axis_size("north")
    owners = east_count * north_count
    photo_count = photos.shape[0]
    slot_total = owners * CAP
    target = footprint[:, 0]
    member_table = (target[:, None] == jnp.arange(owners, dtype=jnp.int32)[None, :]).astype(
        jnp.int32
    )
    earlier_count = jnp.cumsum(member_table, axis=0) - member_table
    place_rank = jnp.sum(earlier_count * member_table, axis=1)
    slot_index = target * CAP + place_rank
    slot_match = slot_index[None, :] == jnp.arange(slot_total, dtype=jnp.int32)[:, None]
    filled = jnp.any(slot_match, axis=1)
    source = jnp.sum(
        jnp.where(slot_match, jnp.arange(photo_count, dtype=jnp.int32)[None, :], 0), axis=1
    )
    record = jnp.stack(
        [
            tile_scale.astype(jnp.float32),
            placement.astype(jnp.float32),
            mask_rows[:, 0].astype(jnp.float32),
            mask_rows[:, 1].astype(jnp.float32),
            jnp.ones((photo_count,), jnp.float32),
        ],
        axis=1,
    ).astype(jnp.bfloat16)
    pixel_total = BANDS * PATCH * PATCH
    payload = jnp.concatenate(
        [
            photos.reshape(photo_count, pixel_total),
            jnp.pad(record, ((0, 0), (0, PATCH - record.shape[1]))),
        ],
        axis=1,
    )
    pick = slot_match.astype(jnp.bfloat16)
    send = jnp.einsum("sp,pj->sj", pick, payload, preferred_element_type=jnp.float32).astype(
        jnp.bfloat16
    )
    got = lax.all_to_all(send, ("east", "north"), split_axis=0, concat_axis=0, tiled=True)
    got_photos = got[:, :pixel_total]
    record_value = got[:, pixel_total : pixel_total + 5].astype(jnp.float32)
    gain_scale = record_value[:, 0]
    block_index = record_value[:, 1].astype(jnp.int32)
    lower_row = record_value[:, 2:3]
    upper_row = record_value[:, 3:4]
    live_flag = record_value[:, 4]
    side_index = jnp.arange(PATCH, dtype=jnp.int32)
    edge_weight = (1 + jnp.minimum(side_index, PATCH - 1 - side_index)).astype(jnp.float32)
    feather = edge_weight[:, None] * edge_weight[None, :] / float((PATCH // 2) ** 2)
    side_float = side_index.astype(jnp.float32)
    inside = ((side_float[None, :] >= lower_row) & (side_float[None, :] < upper_row)).astype(
        jnp.float32
    ) * live_flag[:, None]
    weight = inside[:, :, None] * feather[None, :, :]
    gain_value = gain_scale[:, None, None] * weight
    window_photos = got_photos.reshape(slot_total, BANDS, PATCH, PATCH)
    weighted = window_photos.astype(jnp.float32) * gain_value[:, None, :, :]
    block_match = (block_index[None, :] == jnp.arange(BLOCKS, dtype=jnp.int32)[:, None]).astype(
        jnp.float32
    )
    band_sums = jnp.einsum(
        "bk,kcrs->bcrs",
        block_match,
        weighted,
        precision=lax.Precision.HIGHEST,
        preferred_element_type=jnp.float32,
    )
    weight_sums = jnp.einsum(
        "bk,krs->brs",
        block_match,
        weight,
        precision=lax.Precision.HIGHEST,
        preferred_element_type=jnp.float32,
    )
    summed = jnp.concatenate([band_sums, weight_sums[:, None]], axis=1)
    side_blocks = TILE // PATCH
    strips = []
    for block_row in range(side_blocks):
        strips.append(
            jnp.concatenate(
                [summed[block_row * side_blocks + block_col] for block_col in range(side_blocks)],
                axis=2,
            )
        )
    canvas = jnp.concatenate(strips, axis=1)
    results = []
    east_pos = lax.axis_index("east")
    north_pos = lax.axis_index("north")
    own_levels = [canvas]
    spill_pad = 6
    for depth_step in range(3):
        field = jnp.pad(
            own_levels[-1], ((0, 0), (spill_pad, spill_pad), (spill_pad, spill_pad))
        )
        own_levels.append(
            mask_region(
                reduce_padded(field),
                2,
                TILE >> depth_step + 1,
                north_pos,
                east_pos,
                north_count,
                east_count,
            )
        )
        spill_pad = 4
    stacked = lax.all_gather(own_levels[3][None], ("east", "north"), axis=0, tiled=True)
    true_levels = [canvas] + add_borders(own_levels[1:])
    for depth_step in range(3):
        own_field = true_levels[depth_step]
        if depth_step:
            own_field = crop_margin(own_field, 1, 0)
        laplace_band = normalize(own_field) - expand_padded(normalize(true_levels[depth_step + 1]))
        results.append(laplace_band.astype(jnp.bfloat16))
    whole_field = overlap_add(stacked, east_count, north_count)
    top_field = reduce_padded(jnp.pad(whole_field, ((0, 0), (2, 2), (2, 2))))
    top_normal = normalize(top_field)
    band_three = (
        normalize(whole_field) - expand_padded(jnp.pad(top_normal, ((0, 0), (1, 1), (1, 1))))
    ).astype(jnp.bfloat16)
    apex = top_normal.astype(jnp.bfloat16)
    return (results[0], results[1], results[2], band_three, apex)


def solution(mesh):
    return jax.shard_map(
        body,
        mesh=mesh,
        in_specs=(
            P(("region", "east", "north"), None, None),
            P(("region", "east", "north"), None),
            P(("region", "east", "north")),
            P(("region", "east", "north"), None),
            P(("region", "east", "north")),
        ),
        out_specs=(
            P(None, ("region", "north"), "east"),
            P(None, ("region", "north"), "east"),
            P(None, ("region", "north"), "east"),
            P(None, "region", None),
            P(None, "region", None),
        ),
        check_vma=False,
    )
```

```python
import jax
import jax.numpy as jnp
from jax import lax
from jax.sharding import PartitionSpec as P

BANDS = 4
PATCH = 128
TILE = 512
CAP = 2
BLOCKS = 16


KERNEL = (0.0625, 0.25, 0.375, 0.25, 0.0625)
FLOOR = 0.1
MARGINS = (22, 10, 4, 1)


def padded_2(block, sides, width):
    for axis, dim in sides:
        count = lax.axis_size(axis)
        forward = [(i, i + 1) for i in range(count - 1)]
        backward = [(target, source) for source, target in forward]
        low = lax.ppermute(
            lax.slice_in_dim(block, block.shape[dim] - width, None, axis=dim), axis, forward
        )
        high = lax.ppermute(lax.slice_in_dim(block, 0, width, axis=dim), axis, backward)
        block = jnp.concatenate([low, block, high], axis=dim)
    return block


def tap_table(offset, scale):
    table = jnp.zeros(offset.shape, jnp.float32)
    for tap_index in range(5):
        table = table + jnp.where(offset == tap_index, scale * KERNEL[tap_index], 0.0)
    return table.astype(jnp.bfloat16)


def split_einsum(spec, first, second, table_first):
    field = second if table_first else first
    spread_field = field * 65537.0
    high = spread_field - (spread_field - field)
    low = field - high
    both = jnp.concatenate([high, low], axis=0).astype(jnp.bfloat16)
    pair = (first, both) if table_first else (both, second)
    term = jnp.einsum(spec, *pair, preferred_element_type=jnp.float32)
    chan_count = field.shape[0]
    return term[:chan_count] + term[chan_count:]


def reduce_table(size_in):
    size_out = (size_in - 3) // 2
    out_index = jnp.arange(size_out, dtype=jnp.int32)
    in_index = jnp.arange(size_in, dtype=jnp.int32)
    return tap_table(in_index[None, :] - 2 * out_index[:, None], 1.0)


def expand_table(size_in):
    size_out = 2 * (size_in - 2)
    out_index = jnp.arange(size_out, dtype=jnp.int32)
    in_index = jnp.arange(size_in, dtype=jnp.int32)
    return tap_table(2 * in_index[None, :] - out_index[:, None], 2.0)


def apply_tables(padded, row_table, col_table):
    rows_done = split_einsum("ih,chw->ciw", row_table, padded, True)
    return split_einsum("ciw,jw->cij", rows_done, col_table, False)


def reduce_padded(padded):
    return apply_tables(padded, reduce_table(padded.shape[1]), reduce_table(padded.shape[2]))


def expand_padded(padded):
    return apply_tables(padded, expand_table(padded.shape[1]), expand_table(padded.shape[2]))


def normalize(grid_field):
    return grid_field[:-1] / jnp.maximum(grid_field[-1:], FLOOR)


def crop_margin(grid_field, margin, keep):
    cut = margin - keep
    return grid_field[:, cut : grid_field.shape[1] - cut, cut : grid_field.shape[2] - cut]


def mask_region(grid_field, margin, tile_side, north_pos, east_pos, north_count, east_count):
    row_global = north_pos * tile_side + jnp.arange(grid_field.shape[1], dtype=jnp.int32) - margin
    col_global = east_pos * tile_side + jnp.arange(grid_field.shape[2], dtype=jnp.int32) - margin
    row_keep = (row_global >= 0) & (row_global < north_count * tile_side)
    col_keep = (col_global >= 0) & (col_global < east_count * tile_side)
    keep_table = (row_keep[:, None] & col_keep[None, :]).astype(jnp.float32)
    return grid_field * keep_table[None, :, :]


def add_borders(fields):
    for axis, dim in (("east", 2), ("north", 1)):
        count = lax.axis_size(axis)
        forward = [(i, i + 1) for i in range(count - 1)]
        backward = [(target, source) for source, target in forward]
        other = 3 - dim
        lows = [lax.slice_in_dim(f, f.shape[dim] - 3, f.shape[dim], axis=dim) for f in fields]
        highs = [lax.slice_in_dim(f, 0, 3, axis=dim) for f in fields]
        from_low = lax.ppermute(jnp.concatenate(lows, axis=other), axis, forward)
        from_high = lax.ppermute(jnp.concatenate(highs, axis=other), axis, backward)
        updated = []
        offset = 0
        for f in fields:
            size = f.shape[dim]
            extent = f.shape[other]
            low_part = lax.slice_in_dim(from_low, offset, offset + extent, axis=other)
            high_part = lax.slice_in_dim(from_high, offset, offset + extent, axis=other)
            offset += extent
            pad_low = [(0, 0)] * 3
            pad_high = [(0, 0)] * 3
            pad_low[dim] = (1, size - 4)
            pad_high[dim] = (size - 4, 1)
            updated.append(f + jnp.pad(low_part, pad_low) + jnp.pad(high_part, pad_high))
        fields = updated
    return [crop_margin(f, 2, 1) for f in fields]


def overlap_add(stacked, east_count, north_count):
    chan_count, tall_span, wide_span = stacked.shape[1:]
    tiles = stacked.reshape(east_count, north_count, chan_count, tall_span, wide_span)
    for tile_axis, dim in ((0, 4), (1, 3)):
        span = tiles.shape[dim]
        core = lax.slice_in_dim(tiles, 2, span - 2, axis=dim)
        low_spill = lax.slice_in_dim(tiles, 0, 2, axis=dim)
        high_spill = lax.slice_in_dim(tiles, span - 2, span, axis=dim)
        count = tiles.shape[tile_axis]
        zero = jnp.zeros_like(lax.slice_in_dim(low_spill, 0, 1, axis=tile_axis))
        into_last = jnp.concatenate(
            [lax.slice_in_dim(low_spill, 1, count, axis=tile_axis), zero], axis=tile_axis
        )
        into_first = jnp.concatenate(
            [zero, lax.slice_in_dim(high_spill, 0, count - 1, axis=tile_axis)], axis=tile_axis
        )
        inner = span - 4
        pad_first = [(0, 0)] * 5
        pad_last = [(0, 0)] * 5
        pad_first[dim] = (0, inner - 2)
        pad_last[dim] = (inner - 2, 0)
        tiles = core + jnp.pad(into_first, pad_first) + jnp.pad(into_last, pad_last)
    tall_size, wide_size = tiles.shape[3], tiles.shape[4]
    return tiles.transpose(2, 1, 3, 0, 4).reshape(
        chan_count, north_count * tall_size, east_count * wide_size
    )


def body(photos, footprint, placement, mask_rows, tile_scale):
    east_count = lax.axis_size("east")
    north_count = lax.axis_size("north")
    owners = east_count * north_count
    photo_count = photos.shape[0]
    slot_total = owners * CAP
    target = footprint[:, 0]
    member_table = (target[:, None] == jnp.arange(owners, dtype=jnp.int32)[None, :]).astype(
        jnp.int32
    )
    earlier_count = jnp.cumsum(member_table, axis=0) - member_table
    place_rank = jnp.sum(earlier_count * member_table, axis=1)
    slot_index = target * CAP + place_rank
    slot_match = slot_index[None, :] == jnp.arange(slot_total, dtype=jnp.int32)[:, None]
    filled = jnp.any(slot_match, axis=1)
    source = jnp.sum(
        jnp.where(slot_match, jnp.arange(photo_count, dtype=jnp.int32)[None, :], 0), axis=1
    )
    record = jnp.stack(
        [
            tile_scale.astype(jnp.float32),
            placement.astype(jnp.float32),
            mask_rows[:, 0].astype(jnp.float32),
            mask_rows[:, 1].astype(jnp.float32),
            jnp.ones((photo_count,), jnp.float32),
        ],
        axis=1,
    ).astype(jnp.bfloat16)
    pixel_total = BANDS * PATCH * PATCH
    payload = jnp.concatenate(
        [
            photos.reshape(photo_count, pixel_total),
            jnp.pad(record, ((0, 0), (0, PATCH - record.shape[1]))),
        ],
        axis=1,
    )
    pick = slot_match.astype(jnp.bfloat16)
    send = jnp.einsum("sp,pj->sj", pick, payload, preferred_element_type=jnp.float32).astype(
        jnp.bfloat16
    )
    got = lax.all_to_all(send, ("east", "north"), split_axis=0, concat_axis=0, tiled=True)
    got_photos = got[:, :pixel_total]
    record_value = got[:, pixel_total : pixel_total + 5].astype(jnp.float32)
    gain_scale = record_value[:, 0]
    block_index = record_value[:, 1].astype(jnp.int32)
    lower_row = record_value[:, 2:3]
    upper_row = record_value[:, 3:4]
    live_flag = record_value[:, 4]
    side_index = jnp.arange(PATCH, dtype=jnp.int32)
    edge_weight = (1 + jnp.minimum(side_index, PATCH - 1 - side_index)).astype(jnp.float32)
    feather = edge_weight[:, None] * edge_weight[None, :] / float((PATCH // 2) ** 2)
    side_float = side_index.astype(jnp.float32)
    inside = ((side_float[None, :] >= lower_row) & (side_float[None, :] < upper_row)).astype(
        jnp.float32
    ) * live_flag[:, None]
    weight = inside[:, :, None] * feather[None, :, :]
    gain_value = gain_scale[:, None, None] * weight
    window_photos = got_photos.reshape(slot_total, BANDS, PATCH, PATCH)
    weighted = window_photos.astype(jnp.float32) * gain_value[:, None, :, :]
    block_match = (block_index[None, :] == jnp.arange(BLOCKS, dtype=jnp.int32)[:, None]).astype(
        jnp.float32
    )
    band_sums = jnp.einsum(
        "bk,kcrs->bcrs",
        block_match,
        weighted,
        precision=lax.Precision.HIGHEST,
        preferred_element_type=jnp.float32,
    )
    weight_sums = jnp.einsum(
        "bk,krs->brs",
        block_match,
        weight,
        precision=lax.Precision.HIGHEST,
        preferred_element_type=jnp.float32,
    )
    summed = jnp.concatenate([band_sums, weight_sums[:, None]], axis=1)
    side_blocks = TILE // PATCH
    strips = []
    for block_row in range(side_blocks):
        strips.append(
            jnp.concatenate(
                [summed[block_row * side_blocks + block_col] for block_col in range(side_blocks)],
                axis=2,
            )
        )
    canvas = jnp.concatenate(strips, axis=1)
    results = []
    east_pos = lax.axis_index("east")
    north_pos = lax.axis_index("north")
    own_levels = [canvas]
    spill_pad = 6
    for depth_step in range(3):
        field = jnp.pad(
            own_levels[-1], ((0, 0), (spill_pad, spill_pad), (spill_pad, spill_pad))
        )
        own_levels.append(
            mask_region(
                reduce_padded(field),
                2,
                TILE >> depth_step + 1,
                north_pos,
                east_pos,
                north_count,
                east_count,
            )
        )
        spill_pad = 4
    patch = own_levels[3]
    patch_size = patch.size
    lane_rows = -(-patch_size // 128)
    flat = jnp.pad(patch.reshape(patch_size), (0, lane_rows * 128 - patch_size))
    gathered = lax.all_gather(flat.reshape(1, lane_rows, 128), ("east", "north"), axis=0, tiled=True)
    stacked = gathered.reshape(gathered.shape[0], lane_rows * 128)[:, :patch_size].reshape(
        (gathered.shape[0],) + patch.shape
    )
    true_levels = [canvas] + add_borders(own_levels[1:])
    for depth_step in range(3):
        own_field = true_levels[depth_step]
        if depth_step:
            own_field = crop_margin(own_field, 1, 0)
        laplace_band = normalize(own_field) - expand_padded(normalize(true_levels[depth_step + 1]))
        results.append(laplace_band.astype(jnp.bfloat16))
    whole_field = overlap_add(stacked, east_count, north_count)
    top_field = reduce_padded(jnp.pad(whole_field, ((0, 0), (2, 2), (2, 2))))
    top_normal = normalize(top_field)
    band_three = (
        normalize(whole_field) - expand_padded(jnp.pad(top_normal, ((0, 0), (1, 1), (1, 1))))
    ).astype(jnp.bfloat16)
    apex = top_normal.astype(jnp.bfloat16)
    return (results[0], results[1], results[2], band_three, apex)


def solution(mesh):
    return jax.shard_map(
        body,
        mesh=mesh,
        in_specs=(
            P(("region", "east", "north"), None, None),
            P(("region", "east", "north"), None),
            P(("region", "east", "north")),
            P(("region", "east", "north"), None),
            P(("region", "east", "north")),
        ),
        out_specs=(
            P(None, ("region", "north"), "east"),
            P(None, ("region", "north"), "east"),
            P(None, ("region", "north"), "east"),
            P(None, "region", None),
            P(None, "region", None),
        ),
        check_vma=False,
    )
```

```python
import jax
import jax.numpy as jnp
from jax import lax
from jax.sharding import PartitionSpec as P

BANDS = 4
PATCH = 128
TILE = 512
CAP = 2
BLOCKS = 16


KERNEL = (0.0625, 0.25, 0.375, 0.25, 0.0625)
FLOOR = 0.1
MARGINS = (22, 10, 4, 1)


def padded_2(block, sides, width):
    for axis, dim in sides:
        count = lax.axis_size(axis)
        forward = [(i, i + 1) for i in range(count - 1)]
        backward = [(target, source) for source, target in forward]
        low = lax.ppermute(
            lax.slice_in_dim(block, block.shape[dim] - width, None, axis=dim), axis, forward
        )
        high = lax.ppermute(lax.slice_in_dim(block, 0, width, axis=dim), axis, backward)
        block = jnp.concatenate([low, block, high], axis=dim)
    return block


def tap_table(offset, scale):
    table = jnp.zeros(offset.shape, jnp.float32)
    for tap_index in range(5):
        table = table + jnp.where(offset == tap_index, scale * KERNEL[tap_index], 0.0)
    return table.astype(jnp.bfloat16)


def split_einsum(spec, first, second, table_first):
    field = second if table_first else first
    spread_field = field * 65537.0
    high = spread_field - (spread_field - field)
    low = field - high
    both = jnp.concatenate([high, low], axis=0).astype(jnp.bfloat16)
    pair = (first, both) if table_first else (both, second)
    term = jnp.einsum(spec, *pair, preferred_element_type=jnp.float32)
    chan_count = field.shape[0]
    return term[:chan_count] + term[chan_count:]


def reduce_table(size_in):
    size_out = (size_in - 3) // 2
    out_index = jnp.arange(size_out, dtype=jnp.int32)
    in_index = jnp.arange(size_in, dtype=jnp.int32)
    return tap_table(in_index[None, :] - 2 * out_index[:, None], 1.0)


def expand_table(size_in):
    size_out = 2 * (size_in - 2)
    out_index = jnp.arange(size_out, dtype=jnp.int32)
    in_index = jnp.arange(size_in, dtype=jnp.int32)
    return tap_table(2 * in_index[None, :] - out_index[:, None], 2.0)


def apply_tables(padded, row_table, col_table):
    rows_done = split_einsum("ih,chw->ciw", row_table, padded, True)
    return split_einsum("ciw,jw->cij", rows_done, col_table, False)


def reduce_padded(padded):
    return apply_tables(padded, reduce_table(padded.shape[1]), reduce_table(padded.shape[2]))


def expand_padded(padded):
    return apply_tables(padded, expand_table(padded.shape[1]), expand_table(padded.shape[2]))


def normalize(grid_field):
    return grid_field[:-1] / jnp.maximum(grid_field[-1:], FLOOR)


def crop_margin(grid_field, margin, keep):
    cut = margin - keep
    return grid_field[:, cut : grid_field.shape[1] - cut, cut : grid_field.shape[2] - cut]


def mask_region(grid_field, margin, tile_side, north_pos, east_pos, north_count, east_count):
    row_global = north_pos * tile_side + jnp.arange(grid_field.shape[1], dtype=jnp.int32) - margin
    col_global = east_pos * tile_side + jnp.arange(grid_field.shape[2], dtype=jnp.int32) - margin
    row_keep = (row_global >= 0) & (row_global < north_count * tile_side)
    col_keep = (col_global >= 0) & (col_global < east_count * tile_side)
    keep_table = (row_keep[:, None] & col_keep[None, :]).astype(jnp.float32)
    return grid_field * keep_table[None, :, :]


def add_borders(fields):
    for axis, dim in (("east", 2), ("north", 1)):
        count = lax.axis_size(axis)
        forward = [(i, i + 1) for i in range(count - 1)]
        backward = [(target, source) for source, target in forward]
        other = 3 - dim
        lows = [lax.slice_in_dim(f, f.shape[dim] - 3, f.shape[dim], axis=dim) for f in fields]
        highs = [lax.slice_in_dim(f, 0, 3, axis=dim) for f in fields]
        from_low = lax.ppermute(jnp.concatenate(lows, axis=other), axis, forward)
        from_high = lax.ppermute(jnp.concatenate(highs, axis=other), axis, backward)
        updated = []
        offset = 0
        for f in fields:
            size = f.shape[dim]
            extent = f.shape[other]
            low_part = lax.slice_in_dim(from_low, offset, offset + extent, axis=other)
            high_part = lax.slice_in_dim(from_high, offset, offset + extent, axis=other)
            offset += extent
            pad_low = [(0, 0)] * 3
            pad_high = [(0, 0)] * 3
            pad_low[dim] = (1, size - 4)
            pad_high[dim] = (size - 4, 1)
            updated.append(f + jnp.pad(low_part, pad_low) + jnp.pad(high_part, pad_high))
        fields = updated
    return [crop_margin(f, 2, 1) for f in fields]


def overlap_add(stacked, east_count, north_count):
    chan_count, tall_span, wide_span = stacked.shape[1:]
    tiles = stacked.reshape(east_count, north_count, chan_count, tall_span, wide_span)
    for tile_axis, dim in ((0, 4), (1, 3)):
        span = tiles.shape[dim]
        core = lax.slice_in_dim(tiles, 2, span - 2, axis=dim)
        low_spill = lax.slice_in_dim(tiles, 0, 2, axis=dim)
        high_spill = lax.slice_in_dim(tiles, span - 2, span, axis=dim)
        count = tiles.shape[tile_axis]
        zero = jnp.zeros_like(lax.slice_in_dim(low_spill, 0, 1, axis=tile_axis))
        into_last = jnp.concatenate(
            [lax.slice_in_dim(low_spill, 1, count, axis=tile_axis), zero], axis=tile_axis
        )
        into_first = jnp.concatenate(
            [zero, lax.slice_in_dim(high_spill, 0, count - 1, axis=tile_axis)], axis=tile_axis
        )
        inner = span - 4
        pad_first = [(0, 0)] * 5
        pad_last = [(0, 0)] * 5
        pad_first[dim] = (0, inner - 2)
        pad_last[dim] = (inner - 2, 0)
        tiles = core + jnp.pad(into_first, pad_first) + jnp.pad(into_last, pad_last)
    tall_size, wide_size = tiles.shape[3], tiles.shape[4]
    return tiles.transpose(2, 1, 3, 0, 4).reshape(
        chan_count, north_count * tall_size, east_count * wide_size
    )


def body(photos, footprint, placement, mask_rows, tile_scale):
    east_count = lax.axis_size("east")
    north_count = lax.axis_size("north")
    owners = east_count * north_count
    photo_count = photos.shape[0]
    slot_total = owners * CAP
    target = footprint[:, 0]
    member_table = (target[:, None] == jnp.arange(owners, dtype=jnp.int32)[None, :]).astype(
        jnp.int32
    )
    earlier_count = jnp.cumsum(member_table, axis=0) - member_table
    place_rank = jnp.sum(earlier_count * member_table, axis=1)
    slot_index = target * CAP + place_rank
    slot_match = slot_index[None, :] == jnp.arange(slot_total, dtype=jnp.int32)[:, None]
    filled = jnp.any(slot_match, axis=1)
    source = jnp.sum(
        jnp.where(slot_match, jnp.arange(photo_count, dtype=jnp.int32)[None, :], 0), axis=1
    )
    record = jnp.stack(
        [
            tile_scale.astype(jnp.float32),
            placement.astype(jnp.float32),
            mask_rows[:, 0].astype(jnp.float32),
            mask_rows[:, 1].astype(jnp.float32),
            jnp.ones((photo_count,), jnp.float32),
        ],
        axis=1,
    ).astype(jnp.bfloat16)
    pixel_total = PATCH * PATCH
    record_block = jnp.zeros((photo_count, BANDS, PATCH), jnp.bfloat16)
    record_block = record_block.at[:, 0, : record.shape[1]].set(record)
    payload = jnp.concatenate([photos, record_block], axis=2)
    pick = slot_match.astype(jnp.bfloat16).reshape(owners, CAP, photo_count)
    send = jnp.einsum("osp,pbk->osbk", pick, payload, preferred_element_type=jnp.float32).astype(
        jnp.bfloat16
    )
    got = lax.all_to_all(send, ("east", "north"), split_axis=0, concat_axis=0, tiled=True)
    got = got.reshape(slot_total, BANDS, pixel_total + PATCH)
    got_photos = got[:, :, :pixel_total]
    record_value = got[:, 0, pixel_total : pixel_total + 5].astype(jnp.float32)
    gain_scale = record_value[:, 0]
    block_index = record_value[:, 1].astype(jnp.int32)
    lower_row = record_value[:, 2:3]
    upper_row = record_value[:, 3:4]
    live_flag = record_value[:, 4]
    side_index = jnp.arange(PATCH, dtype=jnp.int32)
    edge_weight = (1 + jnp.minimum(side_index, PATCH - 1 - side_index)).astype(jnp.float32)
    feather = edge_weight[:, None] * edge_weight[None, :] / float((PATCH // 2) ** 2)
    side_float = side_index.astype(jnp.float32)
    inside = ((side_float[None, :] >= lower_row) & (side_float[None, :] < upper_row)).astype(
        jnp.float32
    ) * live_flag[:, None]
    weight = inside[:, :, None] * feather[None, :, :]
    gain_value = gain_scale[:, None, None] * weight
    window_photos = got_photos.reshape(slot_total, BANDS, PATCH, PATCH)
    weighted = window_photos.astype(jnp.float32) * gain_value[:, None, :, :]
    block_match = (block_index[None, :] == jnp.arange(BLOCKS, dtype=jnp.int32)[:, None]).astype(
        jnp.float32
    )
    band_sums = jnp.einsum(
        "bk,kcrs->bcrs",
        block_match,
        weighted,
        precision=lax.Precision.HIGHEST,
        preferred_element_type=jnp.float32,
    )
    weight_sums = jnp.einsum(
        "bk,krs->brs",
        block_match,
        weight,
        precision=lax.Precision.HIGHEST,
        preferred_element_type=jnp.float32,
    )
    summed = jnp.concatenate([band_sums, weight_sums[:, None]], axis=1)
    side_blocks = TILE // PATCH
    strips = []
    for block_row in range(side_blocks):
        strips.append(
            jnp.concatenate(
                [summed[block_row * side_blocks + block_col] for block_col in range(side_blocks)],
                axis=2,
            )
        )
    canvas = jnp.concatenate(strips, axis=1)
    results = []
    east_pos = lax.axis_index("east")
    north_pos = lax.axis_index("north")
    own_levels = [canvas]
    spill_pad = 6
    for depth_step in range(3):
        field = jnp.pad(
            own_levels[-1], ((0, 0), (spill_pad, spill_pad), (spill_pad, spill_pad))
        )
        own_levels.append(
            mask_region(
                reduce_padded(field),
                2,
                TILE >> depth_step + 1,
                north_pos,
                east_pos,
                north_count,
                east_count,
            )
        )
        spill_pad = 4
    stacked = lax.all_gather(own_levels[3][None], ("east", "north"), axis=0, tiled=True)
    true_levels = [canvas] + add_borders(own_levels[1:])
    for depth_step in range(3):
        own_field = true_levels[depth_step]
        if depth_step:
            own_field = crop_margin(own_field, 1, 0)
        laplace_band = normalize(own_field) - expand_padded(normalize(true_levels[depth_step + 1]))
        results.append(laplace_band.astype(jnp.bfloat16))
    whole_field = overlap_add(stacked, east_count, north_count)
    top_field = reduce_padded(jnp.pad(whole_field, ((0, 0), (2, 2), (2, 2))))
    top_normal = normalize(top_field)
    band_three = (
        normalize(whole_field) - expand_padded(jnp.pad(top_normal, ((0, 0), (1, 1), (1, 1))))
    ).astype(jnp.bfloat16)
    apex = top_normal.astype(jnp.bfloat16)
    return (results[0], results[1], results[2], band_three, apex)


def solution(mesh):
    return jax.shard_map(
        body,
        mesh=mesh,
        in_specs=(
            P(("region", "east", "north"), None, None),
            P(("region", "east", "north"), None),
            P(("region", "east", "north")),
            P(("region", "east", "north"), None),
            P(("region", "east", "north")),
        ),
        out_specs=(
            P(None, ("region", "north"), "east"),
            P(None, ("region", "north"), "east"),
            P(None, ("region", "north"), "east"),
            P(None, "region", None),
            P(None, "region", None),
        ),
        check_vma=False,
    )
```

```python
import jax
import jax.numpy as jnp
from jax import lax
from jax.sharding import PartitionSpec as P

BANDS = 4
PATCH = 128
TILE = 512
CAP = 2
BLOCKS = 16


KERNEL = (0.0625, 0.25, 0.375, 0.25, 0.0625)
FLOOR = 0.1
MARGINS = (22, 10, 4, 1)


def padded_2(block, sides, width):
    for axis, dim in sides:
        count = lax.axis_size(axis)
        forward = [(i, i + 1) for i in range(count - 1)]
        backward = [(target, source) for source, target in forward]
        low = lax.ppermute(
            lax.slice_in_dim(block, block.shape[dim] - width, None, axis=dim), axis, forward
        )
        high = lax.ppermute(lax.slice_in_dim(block, 0, width, axis=dim), axis, backward)
        block = jnp.concatenate([low, block, high], axis=dim)
    return block


def tap_table(offset, scale):
    table = jnp.zeros(offset.shape, jnp.float32)
    for tap_index in range(5):
        table = table + jnp.where(offset == tap_index, scale * KERNEL[tap_index], 0.0)
    return table.astype(jnp.bfloat16)


def split_einsum(spec, first, second, table_first):
    field = second if table_first else first
    spread_field = field * 65537.0
    high = spread_field - (spread_field - field)
    low = field - high
    both = jnp.concatenate([high, low], axis=0).astype(jnp.bfloat16)
    pair = (first, both) if table_first else (both, second)
    term = jnp.einsum(spec, *pair, preferred_element_type=jnp.float32)
    chan_count = field.shape[0]
    return term[:chan_count] + term[chan_count:]


def reduce_table(size_in):
    size_out = (size_in - 3) // 2
    out_index = jnp.arange(size_out, dtype=jnp.int32)
    in_index = jnp.arange(size_in, dtype=jnp.int32)
    return tap_table(in_index[None, :] - 2 * out_index[:, None], 1.0)


def expand_table(size_in):
    size_out = 2 * (size_in - 2)
    out_index = jnp.arange(size_out, dtype=jnp.int32)
    in_index = jnp.arange(size_in, dtype=jnp.int32)
    return tap_table(2 * in_index[None, :] - out_index[:, None], 2.0)


def apply_tables(padded, row_table, col_table):
    rows_done = split_einsum("ih,chw->ciw", row_table, padded, True)
    return split_einsum("ciw,jw->cij", rows_done, col_table, False)


def reduce_padded(padded):
    return apply_tables(padded, reduce_table(padded.shape[1]), reduce_table(padded.shape[2]))


def expand_padded(padded):
    return apply_tables(padded, expand_table(padded.shape[1]), expand_table(padded.shape[2]))


def normalize(grid_field):
    return grid_field[:-1] / jnp.maximum(grid_field[-1:], FLOOR)


def crop_margin(grid_field, margin, keep):
    cut = margin - keep
    return grid_field[:, cut : grid_field.shape[1] - cut, cut : grid_field.shape[2] - cut]


def mask_region(grid_field, margin, tile_side, north_pos, east_pos, north_count, east_count):
    row_global = north_pos * tile_side + jnp.arange(grid_field.shape[1], dtype=jnp.int32) - margin
    col_global = east_pos * tile_side + jnp.arange(grid_field.shape[2], dtype=jnp.int32) - margin
    row_keep = (row_global >= 0) & (row_global < north_count * tile_side)
    col_keep = (col_global >= 0) & (col_global < east_count * tile_side)
    keep_table = (row_keep[:, None] & col_keep[None, :]).astype(jnp.float32)
    return grid_field * keep_table[None, :, :]


def add_borders(fields):
    for axis, dim in (("east", 2), ("north", 1)):
        count = lax.axis_size(axis)
        forward = [(i, i + 1) for i in range(count - 1)]
        backward = [(target, source) for source, target in forward]
        other = 3 - dim
        lows = [lax.slice_in_dim(f, f.shape[dim] - 3, f.shape[dim], axis=dim) for f in fields]
        highs = [lax.slice_in_dim(f, 0, 3, axis=dim) for f in fields]
        from_low = lax.ppermute(jnp.concatenate(lows, axis=other), axis, forward)
        from_high = lax.ppermute(jnp.concatenate(highs, axis=other), axis, backward)
        updated = []
        offset = 0
        for f in fields:
            size = f.shape[dim]
            extent = f.shape[other]
            low_part = lax.slice_in_dim(from_low, offset, offset + extent, axis=other)
            high_part = lax.slice_in_dim(from_high, offset, offset + extent, axis=other)
            offset += extent
            pad_low = [(0, 0)] * 3
            pad_high = [(0, 0)] * 3
            pad_low[dim] = (1, size - 4)
            pad_high[dim] = (size - 4, 1)
            updated.append(f + jnp.pad(low_part, pad_low) + jnp.pad(high_part, pad_high))
        fields = updated
    return [crop_margin(f, 2, 1) for f in fields]


def overlap_add(stacked, east_count, north_count):
    chan_count, tall_span, wide_span = stacked.shape[1:]
    tiles = stacked.reshape(east_count, north_count, chan_count, tall_span, wide_span)
    for tile_axis, dim in ((0, 4), (1, 3)):
        span = tiles.shape[dim]
        core = lax.slice_in_dim(tiles, 2, span - 2, axis=dim)
        low_spill = lax.slice_in_dim(tiles, 0, 2, axis=dim)
        high_spill = lax.slice_in_dim(tiles, span - 2, span, axis=dim)
        count = tiles.shape[tile_axis]
        zero = jnp.zeros_like(lax.slice_in_dim(low_spill, 0, 1, axis=tile_axis))
        into_last = jnp.concatenate(
            [lax.slice_in_dim(low_spill, 1, count, axis=tile_axis), zero], axis=tile_axis
        )
        into_first = jnp.concatenate(
            [zero, lax.slice_in_dim(high_spill, 0, count - 1, axis=tile_axis)], axis=tile_axis
        )
        inner = span - 4
        pad_first = [(0, 0)] * 5
        pad_last = [(0, 0)] * 5
        pad_first[dim] = (0, inner - 2)
        pad_last[dim] = (inner - 2, 0)
        tiles = core + jnp.pad(into_first, pad_first) + jnp.pad(into_last, pad_last)
    tall_size, wide_size = tiles.shape[3], tiles.shape[4]
    return tiles.transpose(2, 1, 3, 0, 4).reshape(
        chan_count, north_count * tall_size, east_count * wide_size
    )


def body(photos, footprint, placement, mask_rows, tile_scale):
    east_count = lax.axis_size("east")
    north_count = lax.axis_size("north")
    owners = east_count * north_count
    photo_count = photos.shape[0]
    slot_total = owners * CAP
    target = footprint[:, 0]
    member_table = (target[:, None] == jnp.arange(owners, dtype=jnp.int32)[None, :]).astype(
        jnp.int32
    )
    earlier_count = jnp.cumsum(member_table, axis=0) - member_table
    place_rank = jnp.sum(earlier_count * member_table, axis=1)
    slot_index = target * CAP + place_rank
    slot_match = slot_index[None, :] == jnp.arange(slot_total, dtype=jnp.int32)[:, None]
    filled = jnp.any(slot_match, axis=1)
    source = jnp.sum(
        jnp.where(slot_match, jnp.arange(photo_count, dtype=jnp.int32)[None, :], 0), axis=1
    )
    record = jnp.stack(
        [
            tile_scale.astype(jnp.float32),
            placement.astype(jnp.float32),
            mask_rows[:, 0].astype(jnp.float32),
            mask_rows[:, 1].astype(jnp.float32),
            jnp.ones((photo_count,), jnp.float32),
        ],
        axis=1,
    ).astype(jnp.bfloat16)
    pixel_total = BANDS * PATCH * PATCH
    payload = jnp.concatenate(
        [
            photos.reshape(photo_count, pixel_total),
            jnp.pad(record, ((0, 0), (0, PATCH - record.shape[1]))),
        ],
        axis=1,
    )
    pick = slot_match.astype(jnp.bfloat16)
    send = jnp.einsum("sp,pj->sj", pick, payload, preferred_element_type=jnp.float32).astype(
        jnp.bfloat16
    )
    got = lax.all_to_all(send, ("east", "north"), split_axis=0, concat_axis=0, tiled=True)
    got_photos = got[:, :pixel_total]
    record_value = got[:, pixel_total : pixel_total + 5].astype(jnp.float32)
    gain_scale = record_value[:, 0]
    block_index = record_value[:, 1].astype(jnp.int32)
    lower_row = record_value[:, 2:3]
    upper_row = record_value[:, 3:4]
    live_flag = record_value[:, 4]
    side_index = jnp.arange(PATCH, dtype=jnp.int32)
    edge_weight = (1 + jnp.minimum(side_index, PATCH - 1 - side_index)).astype(jnp.float32)
    feather = edge_weight[:, None] * edge_weight[None, :] / float((PATCH // 2) ** 2)
    side_float = side_index.astype(jnp.float32)
    inside = ((side_float[None, :] >= lower_row) & (side_float[None, :] < upper_row)).astype(
        jnp.float32
    ) * live_flag[:, None]
    weight = inside[:, :, None] * feather[None, :, :]
    gain_value = gain_scale[:, None, None] * weight
    window_photos = got_photos.reshape(slot_total, BANDS, PATCH, PATCH)
    weighted = window_photos.astype(jnp.float32) * gain_value[:, None, :, :]
    block_match = (block_index[None, :] == jnp.arange(BLOCKS, dtype=jnp.int32)[:, None]).astype(
        jnp.float32
    )
    band_sums = jnp.einsum(
        "bk,kcrs->bcrs",
        block_match,
        weighted,
        precision=lax.Precision.HIGHEST,
        preferred_element_type=jnp.float32,
    )
    weight_sums = jnp.einsum(
        "bk,krs->brs",
        block_match,
        weight,
        precision=lax.Precision.HIGHEST,
        preferred_element_type=jnp.float32,
    )
    summed = jnp.concatenate([band_sums, weight_sums[:, None]], axis=1)
    side_blocks = TILE // PATCH
    strips = []
    for block_row in range(side_blocks):
        strips.append(
            jnp.concatenate(
                [summed[block_row * side_blocks + block_col] for block_col in range(side_blocks)],
                axis=2,
            )
        )
    canvas = jnp.concatenate(strips, axis=1)
    results = []
    east_pos = lax.axis_index("east")
    north_pos = lax.axis_index("north")
    own_levels = [canvas]
    spill_pad = 6
    for depth_step in range(3):
        field = jnp.pad(
            own_levels[-1], ((0, 0), (spill_pad, spill_pad), (spill_pad, spill_pad))
        )
        own_levels.append(
            mask_region(
                reduce_padded(field),
                2,
                TILE >> depth_step + 1,
                north_pos,
                east_pos,
                north_count,
                east_count,
            )
        )
        spill_pad = 4
    pair = lax.all_gather(own_levels[3][None], "north", axis=0, tiled=True)
    stacked = lax.all_gather(pair, "east", axis=0, tiled=True)
    true_levels = [canvas] + add_borders(own_levels[1:])
    for depth_step in range(3):
        own_field = true_levels[depth_step]
        if depth_step:
            own_field = crop_margin(own_field, 1, 0)
        laplace_band = normalize(own_field) - expand_padded(normalize(true_levels[depth_step + 1]))
        results.append(laplace_band.astype(jnp.bfloat16))
    whole_field = overlap_add(stacked, east_count, north_count)
    top_field = reduce_padded(jnp.pad(whole_field, ((0, 0), (2, 2), (2, 2))))
    top_normal = normalize(top_field)
    band_three = (
        normalize(whole_field) - expand_padded(jnp.pad(top_normal, ((0, 0), (1, 1), (1, 1))))
    ).astype(jnp.bfloat16)
    apex = top_normal.astype(jnp.bfloat16)
    return (results[0], results[1], results[2], band_three, apex)


def solution(mesh):
    return jax.shard_map(
        body,
        mesh=mesh,
        in_specs=(
            P(("region", "east", "north"), None, None),
            P(("region", "east", "north"), None),
            P(("region", "east", "north")),
            P(("region", "east", "north"), None),
            P(("region", "east", "north")),
        ),
        out_specs=(
            P(None, ("region", "north"), "east"),
            P(None, ("region", "north"), "east"),
            P(None, ("region", "north"), "east"),
            P(None, "region", None),
            P(None, "region", None),
        ),
        check_vma=False,
    )
```

```python
import jax
import jax.numpy as jnp
from jax import lax
from jax.sharding import PartitionSpec as P

BANDS = 4
PATCH = 128
TILE = 512
CAP = 2
BLOCKS = 16


KERNEL = (0.0625, 0.25, 0.375, 0.25, 0.0625)
FLOOR = 0.1
MARGINS = (22, 10, 4, 1)


def padded_2(block, sides, width):
    for axis, dim in sides:
        count = lax.axis_size(axis)
        forward = [(i, i + 1) for i in range(count - 1)]
        backward = [(target, source) for source, target in forward]
        low = lax.ppermute(
            lax.slice_in_dim(block, block.shape[dim] - width, None, axis=dim), axis, forward
        )
        high = lax.ppermute(lax.slice_in_dim(block, 0, width, axis=dim), axis, backward)
        block = jnp.concatenate([low, block, high], axis=dim)
    return block


def tap_table(offset, scale):
    table = jnp.zeros(offset.shape, jnp.float32)
    for tap_index in range(5):
        table = table + jnp.where(offset == tap_index, scale * KERNEL[tap_index], 0.0)
    return table.astype(jnp.bfloat16)


def split_einsum(spec, first, second, table_first):
    field = second if table_first else first
    spread_field = field * 65537.0
    high = spread_field - (spread_field - field)
    low = field - high
    both = jnp.concatenate([high, low], axis=0).astype(jnp.bfloat16)
    pair = (first, both) if table_first else (both, second)
    term = jnp.einsum(spec, *pair, preferred_element_type=jnp.float32)
    chan_count = field.shape[0]
    return term[:chan_count] + term[chan_count:]


def reduce_table(size_in):
    size_out = (size_in - 3) // 2
    out_index = jnp.arange(size_out, dtype=jnp.int32)
    in_index = jnp.arange(size_in, dtype=jnp.int32)
    return tap_table(in_index[None, :] - 2 * out_index[:, None], 1.0)


def expand_table(size_in):
    size_out = 2 * (size_in - 2)
    out_index = jnp.arange(size_out, dtype=jnp.int32)
    in_index = jnp.arange(size_in, dtype=jnp.int32)
    return tap_table(2 * in_index[None, :] - out_index[:, None], 2.0)


def apply_tables(padded, row_table, col_table):
    rows_done = split_einsum("ih,chw->ciw", row_table, padded, True)
    return split_einsum("ciw,jw->cij", rows_done, col_table, False)


def reduce_padded(padded):
    return apply_tables(padded, reduce_table(padded.shape[1]), reduce_table(padded.shape[2]))


def expand_padded(padded):
    return apply_tables(padded, expand_table(padded.shape[1]), expand_table(padded.shape[2]))


def normalize(grid_field):
    return grid_field[:-1] / jnp.maximum(grid_field[-1:], FLOOR)


def crop_margin(grid_field, margin, keep):
    cut = margin - keep
    return grid_field[:, cut : grid_field.shape[1] - cut, cut : grid_field.shape[2] - cut]


def mask_region(grid_field, margin, tile_side, north_pos, east_pos, north_count, east_count):
    row_global = north_pos * tile_side + jnp.arange(grid_field.shape[1], dtype=jnp.int32) - margin
    col_global = east_pos * tile_side + jnp.arange(grid_field.shape[2], dtype=jnp.int32) - margin
    row_keep = (row_global >= 0) & (row_global < north_count * tile_side)
    col_keep = (col_global >= 0) & (col_global < east_count * tile_side)
    keep_table = (row_keep[:, None] & col_keep[None, :]).astype(jnp.float32)
    return grid_field * keep_table[None, :, :]


def add_borders(fields):
    for axis, dim in (("east", 2), ("north", 1)):
        count = lax.axis_size(axis)
        forward = [(i, i + 1) for i in range(count - 1)]
        backward = [(target, source) for source, target in forward]
        other = 3 - dim
        lows = [lax.slice_in_dim(f, f.shape[dim] - 3, f.shape[dim], axis=dim) for f in fields]
        highs = [lax.slice_in_dim(f, 0, 3, axis=dim) for f in fields]
        from_low = lax.ppermute(jnp.concatenate(lows, axis=other), axis, forward)
        from_high = lax.ppermute(jnp.concatenate(highs, axis=other), axis, backward)
        updated = []
        offset = 0
        for f in fields:
            size = f.shape[dim]
            extent = f.shape[other]
            low_part = lax.slice_in_dim(from_low, offset, offset + extent, axis=other)
            high_part = lax.slice_in_dim(from_high, offset, offset + extent, axis=other)
            offset += extent
            pad_low = [(0, 0)] * 3
            pad_high = [(0, 0)] * 3
            pad_low[dim] = (1, size - 4)
            pad_high[dim] = (size - 4, 1)
            updated.append(f + jnp.pad(low_part, pad_low) + jnp.pad(high_part, pad_high))
        fields = updated
    return [crop_margin(f, 2, 1) for f in fields]


def overlap_add(stacked, east_count, north_count):
    chan_count, tall_span, wide_span = stacked.shape[1:]
    tiles = stacked.reshape(east_count, north_count, chan_count, tall_span, wide_span)
    for tile_axis, dim in ((0, 4), (1, 3)):
        span = tiles.shape[dim]
        core = lax.slice_in_dim(tiles, 2, span - 2, axis=dim)
        low_spill = lax.slice_in_dim(tiles, 0, 2, axis=dim)
        high_spill = lax.slice_in_dim(tiles, span - 2, span, axis=dim)
        count = tiles.shape[tile_axis]
        zero = jnp.zeros_like(lax.slice_in_dim(low_spill, 0, 1, axis=tile_axis))
        into_last = jnp.concatenate(
            [lax.slice_in_dim(low_spill, 1, count, axis=tile_axis), zero], axis=tile_axis
        )
        into_first = jnp.concatenate(
            [zero, lax.slice_in_dim(high_spill, 0, count - 1, axis=tile_axis)], axis=tile_axis
        )
        inner = span - 4
        pad_first = [(0, 0)] * 5
        pad_last = [(0, 0)] * 5
        pad_first[dim] = (0, inner - 2)
        pad_last[dim] = (inner - 2, 0)
        tiles = core + jnp.pad(into_first, pad_first) + jnp.pad(into_last, pad_last)
    tall_size, wide_size = tiles.shape[3], tiles.shape[4]
    return tiles.transpose(2, 1, 3, 0, 4).reshape(
        chan_count, north_count * tall_size, east_count * wide_size
    )


def doubling_gather(block, axes):
    for axis, count in reversed(axes):
        position = lax.axis_index(axis)
        step = 1
        while step < count:
            pairs = [(i, i ^ step) for i in range(count)]
            other = lax.ppermute(block, axis, pairs)
            upper = (position // step) % 2 == 1
            first = jnp.where(upper, other, block)
            second = jnp.where(upper, block, other)
            block = jnp.concatenate([first, second], axis=0)
            step *= 2
    return block


def body(photos, footprint, placement, mask_rows, tile_scale):
    east_count = lax.axis_size("east")
    north_count = lax.axis_size("north")
    owners = east_count * north_count
    photo_count = photos.shape[0]
    slot_total = owners * CAP
    target = footprint[:, 0]
    member_table = (target[:, None] == jnp.arange(owners, dtype=jnp.int32)[None, :]).astype(
        jnp.int32
    )
    earlier_count = jnp.cumsum(member_table, axis=0) - member_table
    place_rank = jnp.sum(earlier_count * member_table, axis=1)
    slot_index = target * CAP + place_rank
    slot_match = slot_index[None, :] == jnp.arange(slot_total, dtype=jnp.int32)[:, None]
    filled = jnp.any(slot_match, axis=1)
    source = jnp.sum(
        jnp.where(slot_match, jnp.arange(photo_count, dtype=jnp.int32)[None, :], 0), axis=1
    )
    record = jnp.stack(
        [
            tile_scale.astype(jnp.float32),
            placement.astype(jnp.float32),
            mask_rows[:, 0].astype(jnp.float32),
            mask_rows[:, 1].astype(jnp.float32),
            jnp.ones((photo_count,), jnp.float32),
        ],
        axis=1,
    ).astype(jnp.bfloat16)
    pixel_total = BANDS * PATCH * PATCH
    payload = jnp.concatenate(
        [
            photos.reshape(photo_count, pixel_total),
            jnp.pad(record, ((0, 0), (0, PATCH - record.shape[1]))),
        ],
        axis=1,
    )
    pick = slot_match.astype(jnp.bfloat16)
    send = jnp.einsum("sp,pj->sj", pick, payload, preferred_element_type=jnp.float32).astype(
        jnp.bfloat16
    )
    got = lax.all_to_all(send, ("east", "north"), split_axis=0, concat_axis=0, tiled=True)
    got_photos = got[:, :pixel_total]
    record_value = got[:, pixel_total : pixel_total + 5].astype(jnp.float32)
    gain_scale = record_value[:, 0]
    block_index = record_value[:, 1].astype(jnp.int32)
    lower_row = record_value[:, 2:3]
    upper_row = record_value[:, 3:4]
    live_flag = record_value[:, 4]
    side_index = jnp.arange(PATCH, dtype=jnp.int32)
    edge_weight = (1 + jnp.minimum(side_index, PATCH - 1 - side_index)).astype(jnp.float32)
    feather = edge_weight[:, None] * edge_weight[None, :] / float((PATCH // 2) ** 2)
    side_float = side_index.astype(jnp.float32)
    inside = ((side_float[None, :] >= lower_row) & (side_float[None, :] < upper_row)).astype(
        jnp.float32
    ) * live_flag[:, None]
    weight = inside[:, :, None] * feather[None, :, :]
    gain_value = gain_scale[:, None, None] * weight
    window_photos = got_photos.reshape(slot_total, BANDS, PATCH, PATCH)
    weighted = window_photos.astype(jnp.float32) * gain_value[:, None, :, :]
    block_match = (block_index[None, :] == jnp.arange(BLOCKS, dtype=jnp.int32)[:, None]).astype(
        jnp.float32
    )
    band_sums = jnp.einsum(
        "bk,kcrs->bcrs",
        block_match,
        weighted,
        precision=lax.Precision.HIGHEST,
        preferred_element_type=jnp.float32,
    )
    weight_sums = jnp.einsum(
        "bk,krs->brs",
        block_match,
        weight,
        precision=lax.Precision.HIGHEST,
        preferred_element_type=jnp.float32,
    )
    summed = jnp.concatenate([band_sums, weight_sums[:, None]], axis=1)
    side_blocks = TILE // PATCH
    strips = []
    for block_row in range(side_blocks):
        strips.append(
            jnp.concatenate(
                [summed[block_row * side_blocks + block_col] for block_col in range(side_blocks)],
                axis=2,
            )
        )
    canvas = jnp.concatenate(strips, axis=1)
    results = []
    east_pos = lax.axis_index("east")
    north_pos = lax.axis_index("north")
    own_levels = [canvas]
    spill_pad = 6
    for depth_step in range(3):
        field = jnp.pad(
            own_levels[-1], ((0, 0), (spill_pad, spill_pad), (spill_pad, spill_pad))
        )
        own_levels.append(
            mask_region(
                reduce_padded(field),
                2,
                TILE >> depth_step + 1,
                north_pos,
                east_pos,
                north_count,
                east_count,
            )
        )
        spill_pad = 4
    stacked = doubling_gather(own_levels[3][None], (("east", east_count), ("north", north_count)))
    true_levels = [canvas] + add_borders(own_levels[1:])
    for depth_step in range(3):
        own_field = true_levels[depth_step]
        if depth_step:
            own_field = crop_margin(own_field, 1, 0)
        laplace_band = normalize(own_field) - expand_padded(normalize(true_levels[depth_step + 1]))
        results.append(laplace_band.astype(jnp.bfloat16))
    whole_field = overlap_add(stacked, east_count, north_count)
    top_field = reduce_padded(jnp.pad(whole_field, ((0, 0), (2, 2), (2, 2))))
    top_normal = normalize(top_field)
    band_three = (
        normalize(whole_field) - expand_padded(jnp.pad(top_normal, ((0, 0), (1, 1), (1, 1))))
    ).astype(jnp.bfloat16)
    apex = top_normal.astype(jnp.bfloat16)
    return (results[0], results[1], results[2], band_three, apex)


def solution(mesh):
    return jax.shard_map(
        body,
        mesh=mesh,
        in_specs=(
            P(("region", "east", "north"), None, None),
            P(("region", "east", "north"), None),
            P(("region", "east", "north")),
            P(("region", "east", "north"), None),
            P(("region", "east", "north")),
        ),
        out_specs=(
            P(None, ("region", "north"), "east"),
            P(None, ("region", "north"), "east"),
            P(None, ("region", "north"), "east"),
            P(None, "region", None),
            P(None, "region", None),
        ),
        check_vma=False,
    )
```

```python
import jax
import jax.numpy as jnp
from jax import lax
from jax.sharding import PartitionSpec as P

BANDS = 4
PATCH = 128
TILE = 512
CAP = 2
BLOCKS = 16


KERNEL = (0.0625, 0.25, 0.375, 0.25, 0.0625)
FLOOR = 0.1
MARGINS = (22, 10, 4, 1)


def padded_2(block, sides, width):
    for axis, dim in sides:
        count = lax.axis_size(axis)
        forward = [(i, i + 1) for i in range(count - 1)]
        backward = [(target, source) for source, target in forward]
        low = lax.ppermute(
            lax.slice_in_dim(block, block.shape[dim] - width, None, axis=dim), axis, forward
        )
        high = lax.ppermute(lax.slice_in_dim(block, 0, width, axis=dim), axis, backward)
        block = jnp.concatenate([low, block, high], axis=dim)
    return block


def tap_table(offset, scale):
    table = jnp.zeros(offset.shape, jnp.float32)
    for tap_index in range(5):
        table = table + jnp.where(offset == tap_index, scale * KERNEL[tap_index], 0.0)
    return table.astype(jnp.bfloat16)


def split_einsum(spec, first, second, table_first):
    field = second if table_first else first
    spread_field = field * 65537.0
    high = spread_field - (spread_field - field)
    low = field - high
    both = jnp.concatenate([high, low], axis=0).astype(jnp.bfloat16)
    pair = (first, both) if table_first else (both, second)
    term = jnp.einsum(spec, *pair, preferred_element_type=jnp.float32)
    chan_count = field.shape[0]
    return term[:chan_count] + term[chan_count:]


def reduce_table(size_in):
    size_out = (size_in - 3) // 2
    out_index = jnp.arange(size_out, dtype=jnp.int32)
    in_index = jnp.arange(size_in, dtype=jnp.int32)
    return tap_table(in_index[None, :] - 2 * out_index[:, None], 1.0)


def expand_table(size_in):
    size_out = 2 * (size_in - 2)
    out_index = jnp.arange(size_out, dtype=jnp.int32)
    in_index = jnp.arange(size_in, dtype=jnp.int32)
    return tap_table(2 * in_index[None, :] - out_index[:, None], 2.0)


def apply_tables(padded, row_table, col_table):
    rows_done = split_einsum("ih,chw->ciw", row_table, padded, True)
    return split_einsum("ciw,jw->cij", rows_done, col_table, False)


def reduce_padded(padded):
    return apply_tables(padded, reduce_table(padded.shape[1]), reduce_table(padded.shape[2]))


def expand_padded(padded):
    return apply_tables(padded, expand_table(padded.shape[1]), expand_table(padded.shape[2]))


def normalize(grid_field):
    return grid_field[:-1] / jnp.maximum(grid_field[-1:], FLOOR)


def crop_margin(grid_field, margin, keep):
    cut = margin - keep
    return grid_field[:, cut : grid_field.shape[1] - cut, cut : grid_field.shape[2] - cut]


def mask_region(grid_field, margin, tile_side, north_pos, east_pos, north_count, east_count):
    row_global = north_pos * tile_side + jnp.arange(grid_field.shape[1], dtype=jnp.int32) - margin
    col_global = east_pos * tile_side + jnp.arange(grid_field.shape[2], dtype=jnp.int32) - margin
    row_keep = (row_global >= 0) & (row_global < north_count * tile_side)
    col_keep = (col_global >= 0) & (col_global < east_count * tile_side)
    keep_table = (row_keep[:, None] & col_keep[None, :]).astype(jnp.float32)
    return grid_field * keep_table[None, :, :]


def add_borders(fields):
    for axis, dim in (("east", 2), ("north", 1)):
        count = lax.axis_size(axis)
        forward = [(i, i + 1) for i in range(count - 1)]
        backward = [(target, source) for source, target in forward]
        other = 3 - dim
        lows = [lax.slice_in_dim(f, f.shape[dim] - 3, f.shape[dim], axis=dim) for f in fields]
        highs = [lax.slice_in_dim(f, 0, 3, axis=dim) for f in fields]
        from_low = lax.ppermute(jnp.concatenate(lows, axis=other), axis, forward)
        from_high = lax.ppermute(jnp.concatenate(highs, axis=other), axis, backward)
        updated = []
        offset = 0
        for f in fields:
            size = f.shape[dim]
            extent = f.shape[other]
            low_part = lax.slice_in_dim(from_low, offset, offset + extent, axis=other)
            high_part = lax.slice_in_dim(from_high, offset, offset + extent, axis=other)
            offset += extent
            pad_low = [(0, 0)] * 3
            pad_high = [(0, 0)] * 3
            pad_low[dim] = (1, size - 4)
            pad_high[dim] = (size - 4, 1)
            updated.append(f + jnp.pad(low_part, pad_low) + jnp.pad(high_part, pad_high))
        fields = updated
    return [crop_margin(f, 2, 1) for f in fields]


def overlap_add(stacked, east_count, north_count):
    chan_count, tall_span, wide_span = stacked.shape[1:]
    tiles = stacked.reshape(east_count, north_count, chan_count, tall_span, wide_span)
    for tile_axis, dim in ((0, 4), (1, 3)):
        span = tiles.shape[dim]
        core = lax.slice_in_dim(tiles, 2, span - 2, axis=dim)
        low_spill = lax.slice_in_dim(tiles, 0, 2, axis=dim)
        high_spill = lax.slice_in_dim(tiles, span - 2, span, axis=dim)
        count = tiles.shape[tile_axis]
        zero = jnp.zeros_like(lax.slice_in_dim(low_spill, 0, 1, axis=tile_axis))
        into_last = jnp.concatenate(
            [lax.slice_in_dim(low_spill, 1, count, axis=tile_axis), zero], axis=tile_axis
        )
        into_first = jnp.concatenate(
            [zero, lax.slice_in_dim(high_spill, 0, count - 1, axis=tile_axis)], axis=tile_axis
        )
        inner = span - 4
        pad_first = [(0, 0)] * 5
        pad_last = [(0, 0)] * 5
        pad_first[dim] = (0, inner - 2)
        pad_last[dim] = (inner - 2, 0)
        tiles = core + jnp.pad(into_first, pad_first) + jnp.pad(into_last, pad_last)
    tall_size, wide_size = tiles.shape[3], tiles.shape[4]
    return tiles.transpose(2, 1, 3, 0, 4).reshape(
        chan_count, north_count * tall_size, east_count * wide_size
    )


def body(photos, footprint, placement, mask_rows, tile_scale):
    east_count = lax.axis_size("east")
    north_count = lax.axis_size("north")
    owners = east_count * north_count
    photo_count = photos.shape[0]
    slot_total = owners * CAP
    target = footprint[:, 0]
    member_table = (target[:, None] == jnp.arange(owners, dtype=jnp.int32)[None, :]).astype(
        jnp.int32
    )
    earlier_count = jnp.cumsum(member_table, axis=0) - member_table
    place_rank = jnp.sum(earlier_count * member_table, axis=1)
    slot_index = target * CAP + place_rank
    slot_match = slot_index[None, :] == jnp.arange(slot_total, dtype=jnp.int32)[:, None]
    filled = jnp.any(slot_match, axis=1)
    source = jnp.sum(
        jnp.where(slot_match, jnp.arange(photo_count, dtype=jnp.int32)[None, :], 0), axis=1
    )
    record = jnp.stack(
        [
            tile_scale.astype(jnp.float32),
            placement.astype(jnp.float32),
            mask_rows[:, 0].astype(jnp.float32),
            mask_rows[:, 1].astype(jnp.float32),
            jnp.ones((photo_count,), jnp.float32),
        ],
        axis=1,
    ).astype(jnp.bfloat16)
    image_rows = BANDS * PATCH
    record_rows = 16
    slot_record = jnp.where(filled[:, None], record[source], jnp.zeros((), jnp.bfloat16))
    record_block = jnp.zeros((slot_total, record_rows, PATCH), jnp.bfloat16)
    record_block = record_block.at[:, 0, : record.shape[1]].set(slot_record)
    send = jnp.concatenate(
        [photos.reshape(photo_count, image_rows, PATCH)[source], record_block], axis=1
    )
    slot_rows = image_rows + record_rows
    send = send.reshape(owners, CAP * slot_rows, PATCH)
    got = lax.all_to_all(send, ("east", "north"), split_axis=0, concat_axis=0, tiled=True)
    got = got.reshape(slot_total, slot_rows, PATCH)
    got_photos = got[:, :image_rows, :]
    record_value = got[:, image_rows, :5].astype(jnp.float32)
    gain_scale = record_value[:, 0]
    block_index = record_value[:, 1].astype(jnp.int32)
    lower_row = record_value[:, 2:3]
    upper_row = record_value[:, 3:4]
    live_flag = record_value[:, 4]
    side_index = jnp.arange(PATCH, dtype=jnp.int32)
    edge_weight = (1 + jnp.minimum(side_index, PATCH - 1 - side_index)).astype(jnp.float32)
    feather = edge_weight[:, None] * edge_weight[None, :] / float((PATCH // 2) ** 2)
    side_float = side_index.astype(jnp.float32)
    inside = ((side_float[None, :] >= lower_row) & (side_float[None, :] < upper_row)).astype(
        jnp.float32
    ) * live_flag[:, None]
    weight = inside[:, :, None] * feather[None, :, :]
    gain_value = gain_scale[:, None, None] * weight
    window_photos = got_photos.reshape(slot_total, BANDS, PATCH, PATCH)
    weighted = window_photos.astype(jnp.float32) * gain_value[:, None, :, :]
    block_match = (block_index[None, :] == jnp.arange(BLOCKS, dtype=jnp.int32)[:, None]).astype(
        jnp.float32
    )
    band_sums = jnp.einsum(
        "bk,kcrs->bcrs",
        block_match,
        weighted,
        precision=lax.Precision.HIGHEST,
        preferred_element_type=jnp.float32,
    )
    weight_sums = jnp.einsum(
        "bk,krs->brs",
        block_match,
        weight,
        precision=lax.Precision.HIGHEST,
        preferred_element_type=jnp.float32,
    )
    summed = jnp.concatenate([band_sums, weight_sums[:, None]], axis=1)
    side_blocks = TILE // PATCH
    strips = []
    for block_row in range(side_blocks):
        strips.append(
            jnp.concatenate(
                [summed[block_row * side_blocks + block_col] for block_col in range(side_blocks)],
                axis=2,
            )
        )
    canvas = jnp.concatenate(strips, axis=1)
    results = []
    east_pos = lax.axis_index("east")
    north_pos = lax.axis_index("north")
    own_levels = [canvas]
    spill_pad = 6
    for depth_step in range(3):
        field = jnp.pad(
            own_levels[-1], ((0, 0), (spill_pad, spill_pad), (spill_pad, spill_pad))
        )
        own_levels.append(
            mask_region(
                reduce_padded(field),
                2,
                TILE >> depth_step + 1,
                north_pos,
                east_pos,
                north_count,
                east_count,
            )
        )
        spill_pad = 4
    stacked = lax.all_gather(own_levels[3][None], ("east", "north"), axis=0, tiled=True)
    true_levels = [canvas] + add_borders(own_levels[1:])
    for depth_step in range(3):
        own_field = true_levels[depth_step]
        if depth_step:
            own_field = crop_margin(own_field, 1, 0)
        laplace_band = normalize(own_field) - expand_padded(normalize(true_levels[depth_step + 1]))
        results.append(laplace_band.astype(jnp.bfloat16))
    whole_field = overlap_add(stacked, east_count, north_count)
    top_field = reduce_padded(jnp.pad(whole_field, ((0, 0), (2, 2), (2, 2))))
    top_normal = normalize(top_field)
    band_three = (
        normalize(whole_field) - expand_padded(jnp.pad(top_normal, ((0, 0), (1, 1), (1, 1))))
    ).astype(jnp.bfloat16)
    apex = top_normal.astype(jnp.bfloat16)
    return (results[0], results[1], results[2], band_three, apex)


def solution(mesh):
    return jax.shard_map(
        body,
        mesh=mesh,
        in_specs=(
            P(("region", "east", "north"), None, None),
            P(("region", "east", "north"), None),
            P(("region", "east", "north")),
            P(("region", "east", "north"), None),
            P(("region", "east", "north")),
        ),
        out_specs=(
            P(None, ("region", "north"), "east"),
            P(None, ("region", "north"), "east"),
            P(None, ("region", "north"), "east"),
            P(None, "region", None),
            P(None, "region", None),
        ),
        check_vma=False,
    )
```

```python
import jax
import jax.numpy as jnp
from jax import lax
from jax.sharding import PartitionSpec as P

BANDS = 4
PATCH = 128
TILE = 512
CAP = 2
BLOCKS = 16


KERNEL = (0.0625, 0.25, 0.375, 0.25, 0.0625)
FLOOR = 0.1
MARGINS = (22, 10, 4, 1)


def padded_2(block, sides, width):
    for axis, dim in sides:
        count = lax.axis_size(axis)
        forward = [(i, i + 1) for i in range(count - 1)]
        backward = [(target, source) for source, target in forward]
        low = lax.ppermute(
            lax.slice_in_dim(block, block.shape[dim] - width, None, axis=dim), axis, forward
        )
        high = lax.ppermute(lax.slice_in_dim(block, 0, width, axis=dim), axis, backward)
        block = jnp.concatenate([low, block, high], axis=dim)
    return block


def tap_table(offset, scale):
    table = jnp.zeros(offset.shape, jnp.float32)
    for tap_index in range(5):
        table = table + jnp.where(offset == tap_index, scale * KERNEL[tap_index], 0.0)
    return table.astype(jnp.bfloat16)


def split_einsum(spec, first, second, table_first):
    field = second if table_first else first
    spread_field = field * 65537.0
    high = spread_field - (spread_field - field)
    low = field - high
    both = jnp.concatenate([high, low], axis=0).astype(jnp.bfloat16)
    pair = (first, both) if table_first else (both, second)
    term = jnp.einsum(spec, *pair, preferred_element_type=jnp.float32)
    chan_count = field.shape[0]
    return term[:chan_count] + term[chan_count:]


def reduce_table(size_in):
    size_out = (size_in - 3) // 2
    out_index = jnp.arange(size_out, dtype=jnp.int32)
    in_index = jnp.arange(size_in, dtype=jnp.int32)
    return tap_table(in_index[None, :] - 2 * out_index[:, None], 1.0)


def expand_table(size_in):
    size_out = 2 * (size_in - 2)
    out_index = jnp.arange(size_out, dtype=jnp.int32)
    in_index = jnp.arange(size_in, dtype=jnp.int32)
    return tap_table(2 * in_index[None, :] - out_index[:, None], 2.0)


def apply_tables(padded, row_table, col_table):
    rows_done = split_einsum("ih,chw->ciw", row_table, padded, True)
    return split_einsum("ciw,jw->cij", rows_done, col_table, False)


def reduce_padded(padded):
    return apply_tables(padded, reduce_table(padded.shape[1]), reduce_table(padded.shape[2]))


def expand_padded(padded):
    return apply_tables(padded, expand_table(padded.shape[1]), expand_table(padded.shape[2]))


def normalize(grid_field):
    return grid_field[:-1] / jnp.maximum(grid_field[-1:], FLOOR)


def crop_margin(grid_field, margin, keep):
    cut = margin - keep
    return grid_field[:, cut : grid_field.shape[1] - cut, cut : grid_field.shape[2] - cut]


def mask_region(grid_field, margin, tile_side, north_pos, east_pos, north_count, east_count):
    row_global = north_pos * tile_side + jnp.arange(grid_field.shape[1], dtype=jnp.int32) - margin
    col_global = east_pos * tile_side + jnp.arange(grid_field.shape[2], dtype=jnp.int32) - margin
    row_keep = (row_global >= 0) & (row_global < north_count * tile_side)
    col_keep = (col_global >= 0) & (col_global < east_count * tile_side)
    keep_table = (row_keep[:, None] & col_keep[None, :]).astype(jnp.float32)
    return grid_field * keep_table[None, :, :]


def add_borders(fields):
    for axis, dim in (("east", 2), ("north", 1)):
        count = lax.axis_size(axis)
        forward = [(i, i + 1) for i in range(count - 1)]
        backward = [(target, source) for source, target in forward]
        other = 3 - dim
        lows = [lax.slice_in_dim(f, f.shape[dim] - 3, f.shape[dim], axis=dim) for f in fields]
        highs = [lax.slice_in_dim(f, 0, 3, axis=dim) for f in fields]
        from_low = lax.ppermute(jnp.concatenate(lows, axis=other), axis, forward)
        from_high = lax.ppermute(jnp.concatenate(highs, axis=other), axis, backward)
        updated = []
        offset = 0
        for f in fields:
            size = f.shape[dim]
            extent = f.shape[other]
            low_part = lax.slice_in_dim(from_low, offset, offset + extent, axis=other)
            high_part = lax.slice_in_dim(from_high, offset, offset + extent, axis=other)
            offset += extent
            pad_low = [(0, 0)] * 3
            pad_high = [(0, 0)] * 3
            pad_low[dim] = (1, size - 4)
            pad_high[dim] = (size - 4, 1)
            updated.append(f + jnp.pad(low_part, pad_low) + jnp.pad(high_part, pad_high))
        fields = updated
    return [crop_margin(f, 2, 1) for f in fields]


def overlap_add(stacked, east_count, north_count):
    chan_count, tall_span, wide_span = stacked.shape[1:]
    tiles = stacked.reshape(east_count, north_count, chan_count, tall_span, wide_span)
    for tile_axis, dim in ((0, 4), (1, 3)):
        span = tiles.shape[dim]
        core = lax.slice_in_dim(tiles, 2, span - 2, axis=dim)
        low_spill = lax.slice_in_dim(tiles, 0, 2, axis=dim)
        high_spill = lax.slice_in_dim(tiles, span - 2, span, axis=dim)
        count = tiles.shape[tile_axis]
        zero = jnp.zeros_like(lax.slice_in_dim(low_spill, 0, 1, axis=tile_axis))
        into_last = jnp.concatenate(
            [lax.slice_in_dim(low_spill, 1, count, axis=tile_axis), zero], axis=tile_axis
        )
        into_first = jnp.concatenate(
            [zero, lax.slice_in_dim(high_spill, 0, count - 1, axis=tile_axis)], axis=tile_axis
        )
        inner = span - 4
        pad_first = [(0, 0)] * 5
        pad_last = [(0, 0)] * 5
        pad_first[dim] = (0, inner - 2)
        pad_last[dim] = (inner - 2, 0)
        tiles = core + jnp.pad(into_first, pad_first) + jnp.pad(into_last, pad_last)
    tall_size, wide_size = tiles.shape[3], tiles.shape[4]
    return tiles.transpose(2, 1, 3, 0, 4).reshape(
        chan_count, north_count * tall_size, east_count * wide_size
    )


def body(photos, footprint, placement, mask_rows, tile_scale):
    east_count = lax.axis_size("east")
    north_count = lax.axis_size("north")
    owners = east_count * north_count
    photo_count = photos.shape[0]
    slot_total = owners * CAP
    target = footprint[:, 0]
    member_table = (target[:, None] == jnp.arange(owners, dtype=jnp.int32)[None, :]).astype(
        jnp.int32
    )
    earlier_count = jnp.cumsum(member_table, axis=0) - member_table
    place_rank = jnp.sum(earlier_count * member_table, axis=1)
    slot_index = target * CAP + place_rank
    slot_match = slot_index[None, :] == jnp.arange(slot_total, dtype=jnp.int32)[:, None]
    filled = jnp.any(slot_match, axis=1)
    source = jnp.sum(
        jnp.where(slot_match, jnp.arange(photo_count, dtype=jnp.int32)[None, :], 0), axis=1
    )
    record = jnp.stack(
        [
            tile_scale.astype(jnp.float32),
            placement.astype(jnp.float32),
            mask_rows[:, 0].astype(jnp.float32),
            mask_rows[:, 1].astype(jnp.float32),
            jnp.ones((photo_count,), jnp.float32),
        ],
        axis=1,
    ).astype(jnp.bfloat16)
    pixel_total = BANDS * PATCH * PATCH
    payload = jnp.concatenate(
        [
            photos.reshape(photo_count, pixel_total),
            jnp.pad(record, ((0, 0), (0, PATCH - record.shape[1]))),
        ],
        axis=1,
    )
    pick = slot_match.astype(jnp.bfloat16)
    send = jnp.einsum("sp,pj->sj", pick, payload, preferred_element_type=jnp.float32).astype(
        jnp.bfloat16
    )
    got = lax.all_to_all(send, ("east", "north"), split_axis=0, concat_axis=0, tiled=True)
    got_photos = got[:, :pixel_total]
    record_value = got[:, pixel_total : pixel_total + 5].astype(jnp.float32)
    gain_scale = record_value[:, 0]
    block_index = record_value[:, 1].astype(jnp.int32)
    lower_row = record_value[:, 2:3]
    upper_row = record_value[:, 3:4]
    live_flag = record_value[:, 4]
    side_index = jnp.arange(PATCH, dtype=jnp.int32)
    edge_weight = (1 + jnp.minimum(side_index, PATCH - 1 - side_index)).astype(jnp.float32)
    feather = edge_weight[:, None] * edge_weight[None, :] / float((PATCH // 2) ** 2)
    side_float = side_index.astype(jnp.float32)
    inside = ((side_float[None, :] >= lower_row) & (side_float[None, :] < upper_row)).astype(
        jnp.float32
    ) * live_flag[:, None]
    weight = inside[:, :, None] * feather[None, :, :]
    gain_value = gain_scale[:, None, None] * weight
    window_photos = got_photos.reshape(slot_total, BANDS, PATCH, PATCH)
    weighted = window_photos.astype(jnp.float32) * gain_value[:, None, :, :]
    block_match = (block_index[None, :] == jnp.arange(BLOCKS, dtype=jnp.int32)[:, None]).astype(
        jnp.float32
    )
    contribution = jnp.concatenate([weighted, weight[:, None]], axis=1)
    pieces = []
    remainder = contribution
    for _ in range(2):
        spread_part = remainder * 65537.0
        high = spread_part - (spread_part - remainder)
        pieces.append(high)
        remainder = remainder - high
    pieces.append(remainder)
    stacked_pieces = jnp.concatenate(pieces, axis=0).astype(jnp.bfloat16)
    match_pieces = jnp.concatenate([block_match] * 3, axis=1).astype(jnp.bfloat16)
    summed = jnp.einsum(
        "bk,kcrs->bcrs", match_pieces, stacked_pieces, preferred_element_type=jnp.float32
    )
    side_blocks = TILE // PATCH
    strips = []
    for block_row in range(side_blocks):
        strips.append(
            jnp.concatenate(
                [summed[block_row * side_blocks + block_col] for block_col in range(side_blocks)],
                axis=2,
            )
        )
    canvas = jnp.concatenate(strips, axis=1)
    results = []
    east_pos = lax.axis_index("east")
    north_pos = lax.axis_index("north")
    own_levels = [canvas]
    spill_pad = 6
    for depth_step in range(3):
        field = jnp.pad(
            own_levels[-1], ((0, 0), (spill_pad, spill_pad), (spill_pad, spill_pad))
        )
        own_levels.append(
            mask_region(
                reduce_padded(field),
                2,
                TILE >> depth_step + 1,
                north_pos,
                east_pos,
                north_count,
                east_count,
            )
        )
        spill_pad = 4
    stacked = lax.all_gather(own_levels[3][None], ("east", "north"), axis=0, tiled=True)
    true_levels = [canvas] + add_borders(own_levels[1:])
    for depth_step in range(3):
        own_field = true_levels[depth_step]
        if depth_step:
            own_field = crop_margin(own_field, 1, 0)
        laplace_band = normalize(own_field) - expand_padded(normalize(true_levels[depth_step + 1]))
        results.append(laplace_band.astype(jnp.bfloat16))
    whole_field = overlap_add(stacked, east_count, north_count)
    top_field = reduce_padded(jnp.pad(whole_field, ((0, 0), (2, 2), (2, 2))))
    top_normal = normalize(top_field)
    band_three = (
        normalize(whole_field) - expand_padded(jnp.pad(top_normal, ((0, 0), (1, 1), (1, 1))))
    ).astype(jnp.bfloat16)
    apex = top_normal.astype(jnp.bfloat16)
    return (results[0], results[1], results[2], band_three, apex)


def solution(mesh):
    return jax.shard_map(
        body,
        mesh=mesh,
        in_specs=(
            P(("region", "east", "north"), None, None),
            P(("region", "east", "north"), None),
            P(("region", "east", "north")),
            P(("region", "east", "north"), None),
            P(("region", "east", "north")),
        ),
        out_specs=(
            P(None, ("region", "north"), "east"),
            P(None, ("region", "north"), "east"),
            P(None, ("region", "north"), "east"),
            P(None, "region", None),
            P(None, "region", None),
        ),
        check_vma=False,
    )
```

```python
import jax
import jax.numpy as jnp
from jax import lax
from jax.sharding import PartitionSpec as P

BANDS = 4
PATCH = 128
TILE = 512
CAP = 2
BLOCKS = 16


KERNEL = (0.0625, 0.25, 0.375, 0.25, 0.0625)
FLOOR = 0.1
MARGINS = (22, 10, 4, 1)


def padded_2(block, sides, width):
    for axis, dim in sides:
        count = lax.axis_size(axis)
        forward = [(i, i + 1) for i in range(count - 1)]
        backward = [(target, source) for source, target in forward]
        low = lax.ppermute(
            lax.slice_in_dim(block, block.shape[dim] - width, None, axis=dim), axis, forward
        )
        high = lax.ppermute(lax.slice_in_dim(block, 0, width, axis=dim), axis, backward)
        block = jnp.concatenate([low, block, high], axis=dim)
    return block


def tap_table(offset, scale):
    table = jnp.zeros(offset.shape, jnp.float32)
    for tap_index in range(5):
        table = table + jnp.where(offset == tap_index, scale * KERNEL[tap_index], 0.0)
    return table.astype(jnp.bfloat16)


def split_einsum(spec, first, second, table_first):
    field = second if table_first else first
    spread_field = field * 65537.0
    high = spread_field - (spread_field - field)
    low = field - high
    both = jnp.concatenate([high, low], axis=0).astype(jnp.bfloat16)
    pair = (first, both) if table_first else (both, second)
    term = jnp.einsum(spec, *pair, preferred_element_type=jnp.float32)
    chan_count = field.shape[0]
    return term[:chan_count] + term[chan_count:]


def reduce_table(size_in):
    size_out = (size_in - 3) // 2
    out_index = jnp.arange(size_out, dtype=jnp.int32)
    in_index = jnp.arange(size_in, dtype=jnp.int32)
    return tap_table(in_index[None, :] - 2 * out_index[:, None], 1.0)


def expand_table(size_in):
    size_out = 2 * (size_in - 2)
    out_index = jnp.arange(size_out, dtype=jnp.int32)
    in_index = jnp.arange(size_in, dtype=jnp.int32)
    return tap_table(2 * in_index[None, :] - out_index[:, None], 2.0)


def apply_tables(padded, row_table, col_table):
    rows_done = split_einsum("ih,chw->ciw", row_table, padded, True)
    return split_einsum("ciw,jw->cij", rows_done, col_table, False)


def reduce_padded(padded):
    return apply_tables(padded, reduce_table(padded.shape[1]), reduce_table(padded.shape[2]))


def expand_padded(padded):
    return apply_tables(padded, expand_table(padded.shape[1]), expand_table(padded.shape[2]))


def normalize(grid_field):
    return grid_field[:-1] / jnp.maximum(grid_field[-1:], FLOOR)


def crop_margin(grid_field, margin, keep):
    cut = margin - keep
    return grid_field[:, cut : grid_field.shape[1] - cut, cut : grid_field.shape[2] - cut]


def mask_region(grid_field, margin, tile_side, north_pos, east_pos, north_count, east_count):
    row_global = north_pos * tile_side + jnp.arange(grid_field.shape[1], dtype=jnp.int32) - margin
    col_global = east_pos * tile_side + jnp.arange(grid_field.shape[2], dtype=jnp.int32) - margin
    row_keep = (row_global >= 0) & (row_global < north_count * tile_side)
    col_keep = (col_global >= 0) & (col_global < east_count * tile_side)
    keep_table = (row_keep[:, None] & col_keep[None, :]).astype(jnp.float32)
    return grid_field * keep_table[None, :, :]


def add_borders(fields):
    for axis, dim in (("east", 2), ("north", 1)):
        count = lax.axis_size(axis)
        forward = [(i, i + 1) for i in range(count - 1)]
        backward = [(target, source) for source, target in forward]
        other = 3 - dim
        lows = [lax.slice_in_dim(f, f.shape[dim] - 8, f.shape[dim], axis=dim) for f in fields]
        highs = [lax.slice_in_dim(f, 0, 8, axis=dim) for f in fields]
        from_low = lax.ppermute(jnp.concatenate(lows, axis=other), axis, forward)
        from_high = lax.ppermute(jnp.concatenate(highs, axis=other), axis, backward)
        updated = []
        offset = 0
        for f in fields:
            size = f.shape[dim]
            extent = f.shape[other]
            low_part = lax.slice_in_dim(from_low, offset, offset + extent, axis=other)
            high_part = lax.slice_in_dim(from_high, offset, offset + extent, axis=other)
            offset += extent
            pad_low = [(0, 0)] * 3
            pad_high = [(0, 0)] * 3
            pad_low[dim] = (0, size - 8)
            pad_high[dim] = (size - 8, 0)
            updated.append(f + jnp.pad(low_part, pad_low) + jnp.pad(high_part, pad_high))
        fields = updated
    return fields


def overlap_add(stacked, east_count, north_count):
    chan_count, tall_span, wide_span = stacked.shape[1:]
    tiles = stacked.reshape(east_count, north_count, chan_count, tall_span, wide_span)
    for tile_axis, dim in ((0, 4), (1, 3)):
        span = tiles.shape[dim]
        core = lax.slice_in_dim(tiles, 2, span - 2, axis=dim)
        low_spill = lax.slice_in_dim(tiles, 0, 2, axis=dim)
        high_spill = lax.slice_in_dim(tiles, span - 2, span, axis=dim)
        count = tiles.shape[tile_axis]
        zero = jnp.zeros_like(lax.slice_in_dim(low_spill, 0, 1, axis=tile_axis))
        into_last = jnp.concatenate(
            [lax.slice_in_dim(low_spill, 1, count, axis=tile_axis), zero], axis=tile_axis
        )
        into_first = jnp.concatenate(
            [zero, lax.slice_in_dim(high_spill, 0, count - 1, axis=tile_axis)], axis=tile_axis
        )
        inner = span - 4
        pad_first = [(0, 0)] * 5
        pad_last = [(0, 0)] * 5
        pad_first[dim] = (0, inner - 2)
        pad_last[dim] = (inner - 2, 0)
        tiles = core + jnp.pad(into_first, pad_first) + jnp.pad(into_last, pad_last)
    tall_size, wide_size = tiles.shape[3], tiles.shape[4]
    return tiles.transpose(2, 1, 3, 0, 4).reshape(
        chan_count, north_count * tall_size, east_count * wide_size
    )


def body(photos, footprint, placement, mask_rows, tile_scale):
    east_count = lax.axis_size("east")
    north_count = lax.axis_size("north")
    owners = east_count * north_count
    photo_count = photos.shape[0]
    slot_total = owners * CAP
    target = footprint[:, 0]
    member_table = (target[:, None] == jnp.arange(owners, dtype=jnp.int32)[None, :]).astype(
        jnp.int32
    )
    earlier_count = jnp.cumsum(member_table, axis=0) - member_table
    place_rank = jnp.sum(earlier_count * member_table, axis=1)
    slot_index = target * CAP + place_rank
    slot_match = slot_index[None, :] == jnp.arange(slot_total, dtype=jnp.int32)[:, None]
    filled = jnp.any(slot_match, axis=1)
    source = jnp.sum(
        jnp.where(slot_match, jnp.arange(photo_count, dtype=jnp.int32)[None, :], 0), axis=1
    )
    record = jnp.stack(
        [
            tile_scale.astype(jnp.float32),
            placement.astype(jnp.float32),
            mask_rows[:, 0].astype(jnp.float32),
            mask_rows[:, 1].astype(jnp.float32),
            jnp.ones((photo_count,), jnp.float32),
        ],
        axis=1,
    ).astype(jnp.bfloat16)
    pixel_total = BANDS * PATCH * PATCH
    payload = jnp.concatenate(
        [
            photos.reshape(photo_count, pixel_total),
            jnp.pad(record, ((0, 0), (0, PATCH - record.shape[1]))),
        ],
        axis=1,
    )
    pick = slot_match.astype(jnp.bfloat16)
    send = jnp.einsum("sp,pj->sj", pick, payload, preferred_element_type=jnp.float32).astype(
        jnp.bfloat16
    )
    got = lax.all_to_all(send, ("east", "north"), split_axis=0, concat_axis=0, tiled=True)
    got_photos = got[:, :pixel_total]
    record_value = got[:, pixel_total : pixel_total + 5].astype(jnp.float32)
    gain_scale = record_value[:, 0]
    block_index = record_value[:, 1].astype(jnp.int32)
    lower_row = record_value[:, 2:3]
    upper_row = record_value[:, 3:4]
    live_flag = record_value[:, 4]
    side_index = jnp.arange(PATCH, dtype=jnp.int32)
    edge_weight = (1 + jnp.minimum(side_index, PATCH - 1 - side_index)).astype(jnp.float32)
    feather = edge_weight[:, None] * edge_weight[None, :] / float((PATCH // 2) ** 2)
    side_float = side_index.astype(jnp.float32)
    inside = ((side_float[None, :] >= lower_row) & (side_float[None, :] < upper_row)).astype(
        jnp.float32
    ) * live_flag[:, None]
    weight = inside[:, :, None] * feather[None, :, :]
    gain_value = gain_scale[:, None, None] * weight
    window_photos = got_photos.reshape(slot_total, BANDS, PATCH, PATCH)
    weighted = window_photos.astype(jnp.float32) * gain_value[:, None, :, :]
    block_match = (block_index[None, :] == jnp.arange(BLOCKS, dtype=jnp.int32)[:, None]).astype(
        jnp.float32
    )
    band_sums = jnp.einsum(
        "bk,kcrs->bcrs",
        block_match,
        weighted,
        precision=lax.Precision.HIGHEST,
        preferred_element_type=jnp.float32,
    )
    weight_sums = jnp.einsum(
        "bk,krs->brs",
        block_match,
        weight,
        precision=lax.Precision.HIGHEST,
        preferred_element_type=jnp.float32,
    )
    summed = jnp.concatenate([band_sums, weight_sums[:, None]], axis=1)
    side_blocks = TILE // PATCH
    strips = []
    for block_row in range(side_blocks):
        strips.append(
            jnp.concatenate(
                [summed[block_row * side_blocks + block_col] for block_col in range(side_blocks)],
                axis=2,
            )
        )
    canvas = jnp.concatenate(strips, axis=1)
    results = []
    east_pos = lax.axis_index("east")
    north_pos = lax.axis_index("north")
    own_levels = [canvas]
    spill_pad = 6
    for depth_step in range(3):
        field = jnp.pad(
            own_levels[-1], ((0, 0), (spill_pad, spill_pad), (spill_pad, spill_pad))
        )
        own_levels.append(
            mask_region(
                reduce_padded(field),
                2,
                TILE >> depth_step + 1,
                north_pos,
                east_pos,
                north_count,
                east_count,
            )
        )
        spill_pad = 4
    wide_levels = add_borders([jnp.pad(f, ((0, 0), (2, 2), (2, 2))) for f in own_levels[1:]])
    true_levels = [canvas] + [crop_margin(f, 4, 1) for f in wide_levels[:2]]
    level_three = wide_levels[2]
    top_field = mask_region(
        reduce_padded(level_three), 1, TILE >> 4, north_pos, east_pos, north_count, east_count
    )
    top_normal = normalize(top_field)
    three_tile = (
        normalize(crop_margin(level_three, 4, 0)) - expand_padded(top_normal)
    ).astype(jnp.bfloat16)
    apex_tile = crop_margin(top_normal, 1, 0).astype(jnp.bfloat16)
    three_side = three_tile.shape[1]
    apex_side = apex_tile.shape[1]
    packed = jnp.concatenate(
        [
            three_tile.reshape(BANDS, three_side * three_side),
            apex_tile.reshape(BANDS, apex_side * apex_side),
        ],
        axis=1,
    )
    gathered = lax.all_gather(packed[None], ("east", "north"), axis=0, tiled=True)
    true_levels.append(crop_margin(level_three, 4, 1))
    for depth_step in range(3):
        own_field = true_levels[depth_step]
        if depth_step:
            own_field = crop_margin(own_field, 1, 0)
        laplace_band = normalize(own_field) - expand_padded(normalize(true_levels[depth_step + 1]))
        results.append(laplace_band.astype(jnp.bfloat16))

    def assemble(flat, side):
        tiles = flat.reshape(east_count, north_count, BANDS, side, side)
        return tiles.transpose(2, 1, 3, 0, 4).reshape(
            BANDS, north_count * side, east_count * side
        )

    band_three = assemble(gathered[:, :, : three_side * three_side], three_side)
    apex = assemble(gathered[:, :, three_side * three_side :], apex_side)
    return (results[0], results[1], results[2], band_three, apex)


def solution(mesh):
    return jax.shard_map(
        body,
        mesh=mesh,
        in_specs=(
            P(("region", "east", "north"), None, None),
            P(("region", "east", "north"), None),
            P(("region", "east", "north")),
            P(("region", "east", "north"), None),
            P(("region", "east", "north")),
        ),
        out_specs=(
            P(None, ("region", "north"), "east"),
            P(None, ("region", "north"), "east"),
            P(None, ("region", "north"), "east"),
            P(None, "region", None),
            P(None, "region", None),
        ),
        check_vma=False,
    )
```

```python
import jax
import jax.numpy as jnp
from jax import lax
from jax.sharding import PartitionSpec as P

BANDS = 4
PATCH = 128
TILE = 512
CAP = 2
BLOCKS = 16


KERNEL = (0.0625, 0.25, 0.375, 0.25, 0.0625)
FLOOR = 0.1
MARGINS = (22, 10, 4, 1)


def padded_2(block, sides, width):
    for axis, dim in sides:
        count = lax.axis_size(axis)
        forward = [(i, i + 1) for i in range(count - 1)]
        backward = [(target, source) for source, target in forward]
        low = lax.ppermute(
            lax.slice_in_dim(block, block.shape[dim] - width, None, axis=dim), axis, forward
        )
        high = lax.ppermute(lax.slice_in_dim(block, 0, width, axis=dim), axis, backward)
        block = jnp.concatenate([low, block, high], axis=dim)
    return block


def tap_table(offset, scale):
    table = jnp.zeros(offset.shape, jnp.float32)
    for tap_index in range(5):
        table = table + jnp.where(offset == tap_index, scale * KERNEL[tap_index], 0.0)
    return table.astype(jnp.bfloat16)


def split_einsum(spec, first, second, table_first):
    field = second if table_first else first
    spread_field = field * 65537.0
    high = spread_field - (spread_field - field)
    low = field - high
    both = jnp.concatenate([high, low], axis=0).astype(jnp.bfloat16)
    pair = (first, both) if table_first else (both, second)
    term = jnp.einsum(spec, *pair, preferred_element_type=jnp.float32)
    chan_count = field.shape[0]
    return term[:chan_count] + term[chan_count:]


def reduce_table(size_in):
    size_out = (size_in - 3) // 2
    out_index = jnp.arange(size_out, dtype=jnp.int32)
    in_index = jnp.arange(size_in, dtype=jnp.int32)
    return tap_table(in_index[None, :] - 2 * out_index[:, None], 1.0)


def expand_table(size_in):
    size_out = 2 * (size_in - 2)
    out_index = jnp.arange(size_out, dtype=jnp.int32)
    in_index = jnp.arange(size_in, dtype=jnp.int32)
    return tap_table(2 * in_index[None, :] - out_index[:, None], 2.0)


def apply_tables(padded, row_table, col_table):
    rows_done = split_einsum("ih,chw->ciw", row_table, padded, True)
    return split_einsum("ciw,jw->cij", rows_done, col_table, False)


def reduce_padded(padded):
    return apply_tables(padded, reduce_table(padded.shape[1]), reduce_table(padded.shape[2]))


def expand_padded(padded):
    return apply_tables(padded, expand_table(padded.shape[1]), expand_table(padded.shape[2]))


def normalize(grid_field):
    return grid_field[:-1] / jnp.maximum(grid_field[-1:], FLOOR)


def crop_margin(grid_field, margin, keep):
    cut = margin - keep
    return grid_field[:, cut : grid_field.shape[1] - cut, cut : grid_field.shape[2] - cut]


def mask_region(grid_field, margin, tile_side, north_pos, east_pos, north_count, east_count):
    row_global = north_pos * tile_side + jnp.arange(grid_field.shape[1], dtype=jnp.int32) - margin
    col_global = east_pos * tile_side + jnp.arange(grid_field.shape[2], dtype=jnp.int32) - margin
    row_keep = (row_global >= 0) & (row_global < north_count * tile_side)
    col_keep = (col_global >= 0) & (col_global < east_count * tile_side)
    keep_table = (row_keep[:, None] & col_keep[None, :]).astype(jnp.float32)
    return grid_field * keep_table[None, :, :]


def add_borders(fields):
    for axis, dim in (("east", 2), ("north", 1)):
        count = lax.axis_size(axis)
        forward = [(i, i + 1) for i in range(count - 1)]
        backward = [(target, source) for source, target in forward]
        other = 3 - dim
        lows = [lax.slice_in_dim(f, f.shape[dim] - 8, f.shape[dim], axis=dim) for f in fields]
        highs = [lax.slice_in_dim(f, 0, 8, axis=dim) for f in fields]
        from_low = lax.ppermute(jnp.concatenate(lows, axis=other), axis, forward)
        from_high = lax.ppermute(jnp.concatenate(highs, axis=other), axis, backward)
        updated = []
        offset = 0
        for f in fields:
            size = f.shape[dim]
            extent = f.shape[other]
            low_part = lax.slice_in_dim(from_low, offset, offset + extent, axis=other)
            high_part = lax.slice_in_dim(from_high, offset, offset + extent, axis=other)
            offset += extent
            pad_low = [(0, 0)] * 3
            pad_high = [(0, 0)] * 3
            pad_low[dim] = (0, size - 8)
            pad_high[dim] = (size - 8, 0)
            updated.append(f + jnp.pad(low_part, pad_low) + jnp.pad(high_part, pad_high))
        fields = updated
    return fields


def overlap_add(stacked, east_count, north_count):
    chan_count, tall_span, wide_span = stacked.shape[1:]
    tiles = stacked.reshape(east_count, north_count, chan_count, tall_span, wide_span)
    for tile_axis, dim in ((0, 4), (1, 3)):
        span = tiles.shape[dim]
        core = lax.slice_in_dim(tiles, 2, span - 2, axis=dim)
        low_spill = lax.slice_in_dim(tiles, 0, 2, axis=dim)
        high_spill = lax.slice_in_dim(tiles, span - 2, span, axis=dim)
        count = tiles.shape[tile_axis]
        zero = jnp.zeros_like(lax.slice_in_dim(low_spill, 0, 1, axis=tile_axis))
        into_last = jnp.concatenate(
            [lax.slice_in_dim(low_spill, 1, count, axis=tile_axis), zero], axis=tile_axis
        )
        into_first = jnp.concatenate(
            [zero, lax.slice_in_dim(high_spill, 0, count - 1, axis=tile_axis)], axis=tile_axis
        )
        inner = span - 4
        pad_first = [(0, 0)] * 5
        pad_last = [(0, 0)] * 5
        pad_first[dim] = (0, inner - 2)
        pad_last[dim] = (inner - 2, 0)
        tiles = core + jnp.pad(into_first, pad_first) + jnp.pad(into_last, pad_last)
    tall_size, wide_size = tiles.shape[3], tiles.shape[4]
    return tiles.transpose(2, 1, 3, 0, 4).reshape(
        chan_count, north_count * tall_size, east_count * wide_size
    )


def body(photos, footprint, placement, mask_rows, tile_scale):
    east_count = lax.axis_size("east")
    north_count = lax.axis_size("north")
    owners = east_count * north_count
    photo_count = photos.shape[0]
    slot_total = owners * CAP
    target = footprint[:, 0]
    member_table = (target[:, None] == jnp.arange(owners, dtype=jnp.int32)[None, :]).astype(
        jnp.int32
    )
    earlier_count = jnp.cumsum(member_table, axis=0) - member_table
    place_rank = jnp.sum(earlier_count * member_table, axis=1)
    slot_index = target * CAP + place_rank
    slot_match = slot_index[None, :] == jnp.arange(slot_total, dtype=jnp.int32)[:, None]
    filled = jnp.any(slot_match, axis=1)
    source = jnp.sum(
        jnp.where(slot_match, jnp.arange(photo_count, dtype=jnp.int32)[None, :], 0), axis=1
    )
    record = jnp.stack(
        [
            tile_scale.astype(jnp.float32),
            placement.astype(jnp.float32),
            mask_rows[:, 0].astype(jnp.float32),
            mask_rows[:, 1].astype(jnp.float32),
            jnp.ones((photo_count,), jnp.float32),
        ],
        axis=1,
    ).astype(jnp.bfloat16)
    pixel_total = BANDS * PATCH * PATCH
    payload = jnp.concatenate(
        [
            photos.reshape(photo_count, pixel_total),
            jnp.pad(record, ((0, 0), (0, PATCH - record.shape[1]))),
        ],
        axis=1,
    )
    pick = slot_match.astype(jnp.bfloat16)
    send = jnp.einsum("sp,pj->sj", pick, payload, preferred_element_type=jnp.float32).astype(
        jnp.bfloat16
    )
    got = lax.all_to_all(send, ("east", "north"), split_axis=0, concat_axis=0, tiled=True)
    got_photos = got[:, :pixel_total]
    record_value = got[:, pixel_total : pixel_total + 5].astype(jnp.float32)
    gain_scale = record_value[:, 0]
    block_index = record_value[:, 1].astype(jnp.int32)
    lower_row = record_value[:, 2:3]
    upper_row = record_value[:, 3:4]
    live_flag = record_value[:, 4]
    side_index = jnp.arange(PATCH, dtype=jnp.int32)
    edge_weight = (1 + jnp.minimum(side_index, PATCH - 1 - side_index)).astype(jnp.float32)
    feather = edge_weight[:, None] * edge_weight[None, :] / float((PATCH // 2) ** 2)
    side_float = side_index.astype(jnp.float32)
    inside = ((side_float[None, :] >= lower_row) & (side_float[None, :] < upper_row)).astype(
        jnp.float32
    ) * live_flag[:, None]
    weight = inside[:, :, None] * feather[None, :, :]
    gain_value = gain_scale[:, None, None] * weight
    window_photos = got_photos.reshape(slot_total, BANDS, PATCH, PATCH)
    weighted = window_photos.astype(jnp.float32) * gain_value[:, None, :, :]
    block_match = (block_index[None, :] == jnp.arange(BLOCKS, dtype=jnp.int32)[:, None]).astype(
        jnp.float32
    )
    band_sums = jnp.einsum(
        "bk,kcrs->bcrs",
        block_match,
        weighted,
        precision=lax.Precision.HIGHEST,
        preferred_element_type=jnp.float32,
    )
    weight_sums = jnp.einsum(
        "bk,krs->brs",
        block_match,
        weight,
        precision=lax.Precision.HIGHEST,
        preferred_element_type=jnp.float32,
    )
    summed = jnp.concatenate([band_sums, weight_sums[:, None]], axis=1)
    side_blocks = TILE // PATCH
    strips = []
    for block_row in range(side_blocks):
        strips.append(
            jnp.concatenate(
                [summed[block_row * side_blocks + block_col] for block_col in range(side_blocks)],
                axis=2,
            )
        )
    canvas = jnp.concatenate(strips, axis=1)
    results = []
    east_pos = lax.axis_index("east")
    north_pos = lax.axis_index("north")
    own_levels = [canvas]
    spill_pad = 6
    for depth_step in range(3):
        field = jnp.pad(
            own_levels[-1], ((0, 0), (spill_pad, spill_pad), (spill_pad, spill_pad))
        )
        own_levels.append(
            mask_region(
                reduce_padded(field),
                2,
                TILE >> depth_step + 1,
                north_pos,
                east_pos,
                north_count,
                east_count,
            )
        )
        spill_pad = 4
    wide_levels = add_borders([jnp.pad(f, ((0, 0), (2, 2), (2, 2))) for f in own_levels[1:]])
    true_levels = [canvas] + [crop_margin(f, 4, 1) for f in wide_levels[:2]]
    level_three = wide_levels[2]
    top_field = mask_region(
        reduce_padded(level_three), 1, TILE >> 4, north_pos, east_pos, north_count, east_count
    )
    top_normal = normalize(top_field)
    three_tile = (
        normalize(crop_margin(level_three, 4, 0)) - expand_padded(top_normal)
    ).astype(jnp.bfloat16)
    apex_tile = crop_margin(top_normal, 1, 0).astype(jnp.bfloat16)
    true_levels.append(crop_margin(level_three, 4, 1))
    for depth_step in range(3):
        own_field = true_levels[depth_step]
        if depth_step:
            own_field = crop_margin(own_field, 1, 0)
        laplace_band = normalize(own_field) - expand_padded(normalize(true_levels[depth_step + 1]))
        results.append(laplace_band.astype(jnp.bfloat16))

    def assemble(tile):
        strip = lax.all_gather(tile, "east", axis=2, tiled=True)
        return lax.all_gather(strip, "north", axis=1, tiled=True)

    band_three = assemble(three_tile)
    apex = assemble(apex_tile)
    return (results[0], results[1], results[2], band_three, apex)


def solution(mesh):
    return jax.shard_map(
        body,
        mesh=mesh,
        in_specs=(
            P(("region", "east", "north"), None, None),
            P(("region", "east", "north"), None),
            P(("region", "east", "north")),
            P(("region", "east", "north"), None),
            P(("region", "east", "north")),
        ),
        out_specs=(
            P(None, ("region", "north"), "east"),
            P(None, ("region", "north"), "east"),
            P(None, ("region", "north"), "east"),
            P(None, "region", None),
            P(None, "region", None),
        ),
        check_vma=False,
    )
```

```python
import jax
import jax.numpy as jnp
from jax import lax
from jax.sharding import PartitionSpec as P

BANDS = 4
PATCH = 128
TILE = 512
CAP = 2
BLOCKS = 16


KERNEL = (0.0625, 0.25, 0.375, 0.25, 0.0625)
FLOOR = 0.1
MARGINS = (22, 10, 4, 1)


def padded_2(block, sides, width):
    for axis, dim in sides:
        count = lax.axis_size(axis)
        forward = [(i, i + 1) for i in range(count - 1)]
        backward = [(target, source) for source, target in forward]
        low = lax.ppermute(
            lax.slice_in_dim(block, block.shape[dim] - width, None, axis=dim), axis, forward
        )
        high = lax.ppermute(lax.slice_in_dim(block, 0, width, axis=dim), axis, backward)
        block = jnp.concatenate([low, block, high], axis=dim)
    return block


def tap_table(offset, scale):
    table = jnp.zeros(offset.shape, jnp.float32)
    for tap_index in range(5):
        table = table + jnp.where(offset == tap_index, scale * KERNEL[tap_index], 0.0)
    return table.astype(jnp.bfloat16)


def split_einsum(spec, first, second, table_first):
    field = second if table_first else first
    spread_field = field * 65537.0
    high = spread_field - (spread_field - field)
    low = field - high
    both = jnp.concatenate([high, low], axis=0).astype(jnp.bfloat16)
    pair = (first, both) if table_first else (both, second)
    term = jnp.einsum(spec, *pair, preferred_element_type=jnp.float32)
    chan_count = field.shape[0]
    return term[:chan_count] + term[chan_count:]


def reduce_table(size_in):
    size_out = (size_in - 3) // 2
    out_index = jnp.arange(size_out, dtype=jnp.int32)
    in_index = jnp.arange(size_in, dtype=jnp.int32)
    return tap_table(in_index[None, :] - 2 * out_index[:, None], 1.0)


def expand_table(size_in):
    size_out = 2 * (size_in - 2)
    out_index = jnp.arange(size_out, dtype=jnp.int32)
    in_index = jnp.arange(size_in, dtype=jnp.int32)
    return tap_table(2 * in_index[None, :] - out_index[:, None], 2.0)


def apply_tables(padded, row_table, col_table):
    rows_done = split_einsum("ih,chw->ciw", row_table, padded, True)
    return split_einsum("ciw,jw->cij", rows_done, col_table, False)


def reduce_padded(padded):
    return apply_tables(padded, reduce_table(padded.shape[1]), reduce_table(padded.shape[2]))


def expand_padded(padded):
    return apply_tables(padded, expand_table(padded.shape[1]), expand_table(padded.shape[2]))


def normalize(grid_field):
    return grid_field[:-1] / jnp.maximum(grid_field[-1:], FLOOR)


def crop_margin(grid_field, margin, keep):
    cut = margin - keep
    return grid_field[:, cut : grid_field.shape[1] - cut, cut : grid_field.shape[2] - cut]


def mask_region(grid_field, margin, tile_side, north_pos, east_pos, north_count, east_count):
    row_global = north_pos * tile_side + jnp.arange(grid_field.shape[1], dtype=jnp.int32) - margin
    col_global = east_pos * tile_side + jnp.arange(grid_field.shape[2], dtype=jnp.int32) - margin
    row_keep = (row_global >= 0) & (row_global < north_count * tile_side)
    col_keep = (col_global >= 0) & (col_global < east_count * tile_side)
    keep_table = (row_keep[:, None] & col_keep[None, :]).astype(jnp.float32)
    return grid_field * keep_table[None, :, :]


def add_borders(fields):
    for axis, dim in (("east", 2), ("north", 1)):
        count = lax.axis_size(axis)
        forward = [(i, i + 1) for i in range(count - 1)]
        backward = [(target, source) for source, target in forward]
        other = 3 - dim
        lows = [lax.slice_in_dim(f, f.shape[dim] - 8, f.shape[dim], axis=dim) for f in fields]
        highs = [lax.slice_in_dim(f, 0, 8, axis=dim) for f in fields]
        from_low = lax.ppermute(jnp.concatenate(lows, axis=other), axis, forward)
        from_high = lax.ppermute(jnp.concatenate(highs, axis=other), axis, backward)
        updated = []
        offset = 0
        for f in fields:
            size = f.shape[dim]
            extent = f.shape[other]
            low_part = lax.slice_in_dim(from_low, offset, offset + extent, axis=other)
            high_part = lax.slice_in_dim(from_high, offset, offset + extent, axis=other)
            offset += extent
            pad_low = [(0, 0)] * 3
            pad_high = [(0, 0)] * 3
            pad_low[dim] = (0, size - 8)
            pad_high[dim] = (size - 8, 0)
            updated.append(f + jnp.pad(low_part, pad_low) + jnp.pad(high_part, pad_high))
        fields = updated
    return fields


def overlap_add(stacked, east_count, north_count):
    chan_count, tall_span, wide_span = stacked.shape[1:]
    tiles = stacked.reshape(east_count, north_count, chan_count, tall_span, wide_span)
    for tile_axis, dim in ((0, 4), (1, 3)):
        span = tiles.shape[dim]
        core = lax.slice_in_dim(tiles, 2, span - 2, axis=dim)
        low_spill = lax.slice_in_dim(tiles, 0, 2, axis=dim)
        high_spill = lax.slice_in_dim(tiles, span - 2, span, axis=dim)
        count = tiles.shape[tile_axis]
        zero = jnp.zeros_like(lax.slice_in_dim(low_spill, 0, 1, axis=tile_axis))
        into_last = jnp.concatenate(
            [lax.slice_in_dim(low_spill, 1, count, axis=tile_axis), zero], axis=tile_axis
        )
        into_first = jnp.concatenate(
            [zero, lax.slice_in_dim(high_spill, 0, count - 1, axis=tile_axis)], axis=tile_axis
        )
        inner = span - 4
        pad_first = [(0, 0)] * 5
        pad_last = [(0, 0)] * 5
        pad_first[dim] = (0, inner - 2)
        pad_last[dim] = (inner - 2, 0)
        tiles = core + jnp.pad(into_first, pad_first) + jnp.pad(into_last, pad_last)
    tall_size, wide_size = tiles.shape[3], tiles.shape[4]
    return tiles.transpose(2, 1, 3, 0, 4).reshape(
        chan_count, north_count * tall_size, east_count * wide_size
    )


def body(photos, footprint, placement, mask_rows, tile_scale):
    east_count = lax.axis_size("east")
    north_count = lax.axis_size("north")
    owners = east_count * north_count
    photo_count = photos.shape[0]
    slot_total = owners * CAP
    target = footprint[:, 0]
    member_table = (target[:, None] == jnp.arange(owners, dtype=jnp.int32)[None, :]).astype(
        jnp.int32
    )
    earlier_count = jnp.cumsum(member_table, axis=0) - member_table
    place_rank = jnp.sum(earlier_count * member_table, axis=1)
    slot_index = target * CAP + place_rank
    slot_match = slot_index[None, :] == jnp.arange(slot_total, dtype=jnp.int32)[:, None]
    filled = jnp.any(slot_match, axis=1)
    source = jnp.sum(
        jnp.where(slot_match, jnp.arange(photo_count, dtype=jnp.int32)[None, :], 0), axis=1
    )
    record = jnp.stack(
        [
            tile_scale.astype(jnp.float32),
            placement.astype(jnp.float32),
            mask_rows[:, 0].astype(jnp.float32),
            mask_rows[:, 1].astype(jnp.float32),
            jnp.ones((photo_count,), jnp.float32),
        ],
        axis=1,
    ).astype(jnp.bfloat16)
    pixel_total = BANDS * PATCH * PATCH
    payload = jnp.concatenate(
        [
            photos.reshape(photo_count, pixel_total),
            jnp.pad(record, ((0, 0), (0, PATCH - record.shape[1]))),
        ],
        axis=1,
    )
    pick = slot_match.astype(jnp.bfloat16)
    send = jnp.einsum("sp,pj->sj", pick, payload, preferred_element_type=jnp.float32).astype(
        jnp.bfloat16
    )
    got = lax.all_to_all(send, ("east", "north"), split_axis=0, concat_axis=0, tiled=True)
    got_photos = got[:, :pixel_total]
    record_value = got[:, pixel_total : pixel_total + 5].astype(jnp.float32)
    gain_scale = record_value[:, 0]
    block_index = record_value[:, 1].astype(jnp.int32)
    lower_row = record_value[:, 2:3]
    upper_row = record_value[:, 3:4]
    live_flag = record_value[:, 4]
    side_index = jnp.arange(PATCH, dtype=jnp.int32)
    edge_weight = (1 + jnp.minimum(side_index, PATCH - 1 - side_index)).astype(jnp.float32)
    feather = edge_weight[:, None] * edge_weight[None, :] / float((PATCH // 2) ** 2)
    side_float = side_index.astype(jnp.float32)
    inside = ((side_float[None, :] >= lower_row) & (side_float[None, :] < upper_row)).astype(
        jnp.float32
    ) * live_flag[:, None]
    weight = inside[:, :, None] * feather[None, :, :]
    gain_value = gain_scale[:, None, None] * weight
    window_photos = got_photos.reshape(slot_total, BANDS, PATCH, PATCH)
    weighted = window_photos.astype(jnp.float32) * gain_value[:, None, :, :]
    block_match = (block_index[None, :] == jnp.arange(BLOCKS, dtype=jnp.int32)[:, None]).astype(
        jnp.float32
    )
    band_sums = jnp.einsum(
        "bk,kcrs->bcrs",
        block_match,
        weighted,
        precision=lax.Precision.HIGHEST,
        preferred_element_type=jnp.float32,
    )
    weight_sums = jnp.einsum(
        "bk,krs->brs",
        block_match,
        weight,
        precision=lax.Precision.HIGHEST,
        preferred_element_type=jnp.float32,
    )
    summed = jnp.concatenate([band_sums, weight_sums[:, None]], axis=1)
    side_blocks = TILE // PATCH
    strips = []
    for block_row in range(side_blocks):
        strips.append(
            jnp.concatenate(
                [summed[block_row * side_blocks + block_col] for block_col in range(side_blocks)],
                axis=2,
            )
        )
    canvas = jnp.concatenate(strips, axis=1)
    results = []
    east_pos = lax.axis_index("east")
    north_pos = lax.axis_index("north")
    own_levels = [canvas]
    spill_pad = 6
    for depth_step in range(3):
        field = jnp.pad(
            own_levels[-1], ((0, 0), (spill_pad, spill_pad), (spill_pad, spill_pad))
        )
        own_levels.append(
            mask_region(
                reduce_padded(field),
                2,
                TILE >> depth_step + 1,
                north_pos,
                east_pos,
                north_count,
                east_count,
            )
        )
        spill_pad = 4
    wide_levels = add_borders([jnp.pad(f, ((0, 0), (2, 2), (2, 2))) for f in own_levels[1:]])
    true_levels = [canvas] + [crop_margin(f, 4, 1) for f in wide_levels[:2]]
    level_three = wide_levels[2]
    top_field = mask_region(
        reduce_padded(level_three), 1, TILE >> 4, north_pos, east_pos, north_count, east_count
    )
    top_normal = normalize(top_field)
    three_tile = (
        normalize(crop_margin(level_three, 4, 0)) - expand_padded(top_normal)
    ).astype(jnp.bfloat16)
    apex_tile = crop_margin(top_normal, 1, 0).astype(jnp.bfloat16)
    three_side = three_tile.shape[1]
    apex_side = apex_tile.shape[1]
    packed = jnp.concatenate(
        [
            three_tile.reshape(BANDS, three_side * three_side),
            apex_tile.reshape(BANDS, apex_side * apex_side),
        ],
        axis=1,
    )
    packed_rows = packed.size // PATCH
    gathered = lax.all_gather(
        packed.reshape(1, packed_rows, PATCH), ("east", "north"), axis=0, tiled=True
    ).reshape((-1,) + packed.shape)
    true_levels.append(crop_margin(level_three, 4, 1))
    for depth_step in range(3):
        own_field = true_levels[depth_step]
        if depth_step:
            own_field = crop_margin(own_field, 1, 0)
        laplace_band = normalize(own_field) - expand_padded(normalize(true_levels[depth_step + 1]))
        results.append(laplace_band.astype(jnp.bfloat16))

    def assemble(flat, side):
        tiles = flat.reshape(east_count, north_count, BANDS, side, side)
        return tiles.transpose(2, 1, 3, 0, 4).reshape(
            BANDS, north_count * side, east_count * side
        )

    band_three = assemble(gathered[:, :, : three_side * three_side], three_side)
    apex = assemble(gathered[:, :, three_side * three_side :], apex_side)
    return (results[0], results[1], results[2], band_three, apex)


def solution(mesh):
    return jax.shard_map(
        body,
        mesh=mesh,
        in_specs=(
            P(("region", "east", "north"), None, None),
            P(("region", "east", "north"), None),
            P(("region", "east", "north")),
            P(("region", "east", "north"), None),
            P(("region", "east", "north")),
        ),
        out_specs=(
            P(None, ("region", "north"), "east"),
            P(None, ("region", "north"), "east"),
            P(None, ("region", "north"), "east"),
            P(None, "region", None),
            P(None, "region", None),
        ),
        check_vma=False,
    )
```
